128 devices in a mesh: area: 128 (over x, z, y, core).
Axes of the slice: x: 4, y: 4, z: 4, core: 2. Of those that a mesh axis runs over, the one named last changes fastest.
Arguments:
- population: float32 [2048, 96, 1024], P('area'), may hold values from 0.1 to 10
- area_target: float32 [2048, 96], P('area'), may hold values from 500 to 5000
- national_target: float32 [96, 32], replicated, may hold values from 50000 to 500000
- zone_target: float32 [1024, 1536], P('area'), may hold values from 500 to 10000
- area_zone: int32 [2048], P('area'), may hold values from 0 to 1023, never falling along the last dimension, each value on 1 to 6 neighbouring positions
- zone_order: int32 [1024], replicated, may hold values from 0 to 1023, each once
Outputs:
- fitted: float32 [2048, 96, 1024], P('area')
The draws below stay inside these ranges and needn't reach their ends.
Inputs may be any that keep to these rules, and one draw needn't show every extreme that they name: area_zone never falls along the areas; every zone holds 1 to 6 areas, and some zone exactly 6. `zone_order`: every zone appears once.
All inputs are finite; a program needn't handle non-finite values.
Results may differ from the reference program's by a relative error of at most 0.0001.
Values sent between devices are 32-bit elements; how exact they have to be, the bound alone decides.
No kernel may reach another device: no remote copies, remote signals or barrier semaphores. Data moves between devices by JAX's collectives and lax.ppermute only.
A program may use at most 128 MiB of HBM per device.

```python
import math
import jax
import jax.numpy as jnp
import numpy as np

AGE = 48
SEX = 2
INC = 32
HH = 8
TU = 4
AREAS = 2048
ZONES = 1024
ZONE_MOST = 6


def shard_levels(own_key, dims, cuts, smallest, high):
    gain = 1.0
    for position, shards_of in cuts:
        draws = jax.random.uniform(jax.random.fold_in(jax.random.fold_in(own_key, 6), position), (shards_of,), jnp.float32, smallest / len(cuts), high / len(cuts))
        gain = gain * jnp.repeat(jnp.exp(draws), dims[position] // shards_of).reshape((-1,) + (1,) * (len(dims) - 1 - position))
    return gain


def split_up(number_of, total, limit, skew):
    weights = [(1 << 20) // math.isqrt(grade ** skew) + 1 for grade in range(2, number_of + 1)]
    spare, given = total - limit - (number_of - 1), [1] * (number_of - 1)
    while spare > 0:
        movable = [i for i in range(number_of - 1) if given[i] < limit]
        whole, left = sum([weights[i] for i in movable]), spare
        for i in movable:
            addition = min(limit - given[i], max(1, left * weights[i] // whole), spare)
            given[i] = given[i] + addition
            spare = spare - addition
    return np.array([limit] + given)


def uneven_parts(own_key, number_of, total, reach, skew):
    if number_of == 2:
        one = jax.random.randint(own_key, (), max(1, total - reach), min(reach, total - 1) + 1)
        return jnp.stack([one, total - one])
    sizes = jnp.asarray(split_up(number_of, total, reach, skew), jnp.int32)
    couples = (number_of - 1) // 2
    donor, receiver = sizes[1:1 + 2 * couples:2], sizes[2:2 + 2 * couples:2]
    margin = jnp.minimum(donor - 1, reach - receiver)
    moved = jax.random.randint(jax.random.fold_in(own_key, 1), (couples,), 0, 1 << 20) % (margin + 1)
    sizes = sizes.at[1:1 + 2 * couples:2].set(donor - moved).at[2:2 + 2 * couples:2].set(receiver + moved)
    return sizes[jax.random.permutation(jax.random.fold_in(own_key, 2), number_of)]


def setup_inputs(seed: int = 0) -> dict:
    arg_keys = jax.random.split(jax.random.key(seed), 7)
    return {
        "population": jnp.clip(jnp.exp(math.log(10.0) - 4.6051702 * jax.random.uniform(arg_keys[0], (AREAS, AGE * SEX, INC * HH * TU), jnp.float32) ** shard_levels(arg_keys[0], (AREAS, AGE * SEX, INC * HH * TU), ((0, 128),), -0.2, 0.2)), 0.1, 10.0),
        "area_target": jnp.clip(jnp.exp(math.log(5000.0) - 2.3025851 * jax.random.uniform(arg_keys[1], (AREAS, AGE * SEX), jnp.float32) ** shard_levels(arg_keys[1], (AREAS, AGE * SEX), ((0, 128),), -0.2, 0.2)), 500.0, 5000.0),
        "national_target": jnp.clip(jnp.exp(jax.random.uniform(arg_keys[2], (AGE * SEX, HH * TU), jnp.float32, math.log(50000.0), math.log(500000.0))), 50000.0, 500000.0),
        "zone_target": jnp.clip(jnp.exp(math.log(10000.0) - 2.9957323 * jax.random.uniform(arg_keys[3], (ZONES, AGE * INC), jnp.float32) ** shard_levels(arg_keys[3], (ZONES, AGE * INC), ((0, 128),), -0.2, 0.2)), 500.0, 10000.0),
        "area_zone": jnp.searchsorted(jnp.cumsum(uneven_parts(arg_keys[4], ZONES, AREAS, ZONE_MOST, 2)), jnp.arange(AREAS), side="right").astype(jnp.int32),
        "zone_order": jax.random.permutation(arg_keys[5], ZONES).astype(jnp.int32),
    }


def reference(population, area_target, national_target, zone_target, area_zone, zone_order):
    count = population.shape[0]
    area_sum = jnp.sum(population, axis=2)
    first = population * (area_target / area_sum)[:, :, None]
    view = first.reshape(count, AGE * SEX, INC, HH * TU)
    national = jnp.sum(view, axis=(0, 2))
    second = view * (national_target / national)[None, :, None, :]
    split = second.reshape(count, AGE, SEX, INC, HH * TU)
    area_margin = jnp.sum(split, axis=(2, 4)).reshape(count, AGE * INC)
    zone_sum = jax.ops.segment_sum(area_margin, area_zone, num_segments=ZONES)
    targets = jnp.zeros_like(zone_sum).at[zone_order].set(zone_target)
    zone_ratio = targets / zone_sum
    factor = zone_ratio[area_zone].reshape(count, AGE, 1, INC, 1)
    return (split * factor).reshape(count, AGE * SEX, INC * HH * TU)
```

```python
import jax
import jax.numpy as jnp
from jax import lax
from jax.sharding import PartitionSpec as P

AGE = 48
SEX = 2
INC = 32
HH = 8
TU = 4
ZONE_MOST = 6
GROUP = 16


def _shift(x, n, group, k):
    perm = [(i, (i // group) * group + (i % group + k) % group) for i in range(n)]
    return lax.ppermute(x, "area", perm)


def _across(x, n, group, j):
    groups = n // group
    perm = [(i, ((i // group + j) % groups) * group + i % group) for i in range(n)]
    return lax.ppermute(x, "area", perm)


def make_body(n):
    groups = n // GROUP

    def body(population, area_target, national_target, zone_target, area_zone, zone_order):
        count = population.shape[0]
        rows = zone_target.shape[0]
        zones = zone_order.shape[0]
        cols = zone_target.shape[1]
        most = count
        assert ZONE_MOST < count
        idx = lax.axis_index("area")
        grp, pos = idx // GROUP, idx % GROUP
        f32 = jnp.float32

        labels = jnp.arange(zones, dtype=jnp.int32)
        slot_of = jnp.zeros((zones,), jnp.int32).at[zone_order].set(labels)
        zlo = area_zone[0]
        zhi = area_zone[count - 1]
        ks = jnp.arange(most, dtype=jnp.int32)
        kz = zlo + ks
        valid = kz <= zhi
        slot = slot_of[jnp.minimum(kz, zones - 1)]
        owner_grp = slot // (rows * GROUP)
        j_k = (owner_grp - grp) % groups
        member = (slot // rows) % GROUP
        pidx = ((pos - member) % GROUP) * rows + slot % rows
        same = (j_k[:, None] == j_k[None, :]) & valid[None, :] & (ks[None, :] < ks[:, None])
        q_k = jnp.sum(same.astype(jnp.int32), axis=1)
        req = jnp.zeros((groups, most), jnp.int32).at[jnp.where(valid, j_k, groups), q_k].set(pidx, mode="drop")

        pool = [zone_target]
        for k in range(1, GROUP):
            pool.append(_shift(zone_target, n, GROUP, k))
        pool = jnp.concatenate(pool, axis=0)
        asked = [req[0]]
        for j in range(1, groups):
            asked.append(_across(req[j], n, GROUP, j))
        replies = [jnp.take(pool, req[0], axis=0)]
        for j in range(1, groups):
            replies.append(_across(jnp.take(pool, asked[j], axis=0), n, GROUP, -j))
        reply = jnp.stack(replies)
        target = reply[j_k, q_k]

        right = [(i, i + 1) for i in range(n - 1)]
        left = [(i, i - 1) for i in range(1, n)]
        zhi_left = lax.ppermute(zhi[None], "area", right)[0]
        zlo_right = lax.ppermute(zlo[None], "area", left)[0]

        view = population.reshape(count, AGE * SEX, INC, HH * TU)
        t1 = jnp.sum(view, axis=2)
        area_sum = jnp.sum(t1, axis=2)
        s1 = area_target / area_sum
        part = jnp.sum(t1 * s1[:, :, None], axis=0)
        acc = part
        for k in range(1, GROUP):
            acc = acc + _shift(part, n, GROUP, k)
        national = acc
        for j in range(1, groups):
            national = national + _across(acc, n, GROUP, j)
        s2 = national_target / national

        w = s1[:, :, None] * s2[None, :, :]
        am = jnp.sum(view * w[:, :, None, :], axis=3)
        am = jnp.sum(am.reshape(count, AGE, SEX, INC), axis=2).reshape(count, AGE * INC)
        k_a = area_zone - zlo
        onehot = (k_a[:, None] == ks[None, :]).astype(f32)
        zp = jnp.sum(onehot[:, :, None] * am[:, None, :], axis=0)
        nk = zhi - zlo
        from_left = lax.ppermute(zp[nk], "area", right)
        from_right = lax.ppermute(zp[0], "area", left)
        zp = zp.at[0].add(jnp.where(zhi_left == zlo, from_left, 0.0))
        zp = zp.at[nk].add(jnp.where(zlo_right == zhi, from_right, 0.0))
        ratio = target / zp
        ratio_a = jnp.take(ratio, k_a, axis=0)

        fac = (w.reshape(count, AGE, SEX, 1, HH * TU)
               * ratio_a.reshape(count, AGE, 1, INC, 1))
        out = population.reshape(count, AGE, SEX, INC, HH * TU) * fac
        return out.reshape(count, AGE * SEX, INC * HH * TU)

    return body


def solution(mesh):
    n = mesh.shape["area"]
    placed = (P("area", None, None), P("area", None), P(), P("area", None), P("area"), P())
    return jax.shard_map(
        make_body(n), mesh=mesh, in_specs=placed, out_specs=P("area", None, None), check_vma=False
    )
```

```python
import jax
import jax.numpy as jnp
import numpy as np
from jax import lax
from jax.sharding import Mesh, PartitionSpec as P

AGE = 48
SEX = 2
INC = 32
HH = 8
TU = 4
ZONE_MOST = 6
MEMBERS = 8
ROOMY = 5
AXES = ("col", "mem")


def _xor(x, n, bit):
    return lax.ppermute(x, AXES, [(i, i ^ bit) for i in range(n)])


def make_body(n):
    cols = n // MEMBERS

    def body(population, area_target, national_target, zone_target, area_zone, zone_order):
        count = population.shape[0]
        rows = zone_target.shape[0]
        zones = zone_order.shape[0]
        width = zone_target.shape[1]
        most = count
        pool_rows = rows * MEMBERS
        assert ZONE_MOST < count and (AGE * SEX * HH * TU) % width == 0 and 2 * cols <= width
        f32 = jnp.float32
        idx = lax.axis_index(AXES)
        col, mem = idx // MEMBERS, idx % MEMBERS

        labels = jnp.arange(zones, dtype=jnp.int32)
        slot_of = jnp.zeros((zones,), jnp.int32).at[zone_order].set(labels)
        zlo = area_zone[0]
        zhi = area_zone[count - 1]
        ks = jnp.arange(most, dtype=jnp.int32)
        lanes = jnp.arange(width, dtype=jnp.int32)

        view = population.reshape(count, AGE * SEX, INC, HH * TU)
        t1 = jnp.sum(view, axis=2)
        area_sum = jnp.sum(t1, axis=2)
        s1 = area_target / area_sum
        part = jnp.sum(t1 * s1[:, :, None], axis=0)
        nat_rows = (AGE * SEX * HH * TU) // width

        zrow = jnp.where(lanes == 2 * col, zlo.astype(f32), 0.0) + jnp.where(lanes == 2 * col + 1, zhi.astype(f32), 0.0)
        msg = jnp.concatenate([part.reshape(nat_rows, width), zrow[None]], axis=0)
        bit = MEMBERS
        while bit < n:
            msg = msg + _xor(msg, n, bit)
            bit *= 2
        nat = msg[:nat_rows]
        zinfo = msg[nat_rows, : 2 * cols].reshape(cols, 2).astype(jnp.int32)

        c_kz = zinfo[:, 0:1] + ks[None, :]
        c_valid = c_kz <= zinfo[:, 1:2]
        c_slot = slot_of[jnp.minimum(c_kz, zones - 1)]
        c_grp = c_slot // pool_rows
        earlier = (c_grp[:, :, None] == c_grp[:, None, :]) & c_valid[:, None, :] & (ks[None, None, :] < ks[None, :, None])
        c_rank = jnp.sum(earlier.astype(jnp.int32), axis=2)
        over = jnp.any(c_valid & (c_rank >= ROOMY)).astype(f32)

        pool = zone_target
        flag = jnp.where(lanes == 0, over, 0.0)[None]
        bit = 1
        while bit < MEMBERS:
            msg = jnp.concatenate([nat, flag, pool], axis=0)
            got = _xor(msg, n, bit)
            nat = nat + got[:nat_rows]
            flag = flag + got[nat_rows:nat_rows + 1]
            theirs = got[nat_rows + 1:]
            pool = jnp.where((mem & bit) == 0, jnp.concatenate([pool, theirs], 0), jnp.concatenate([theirs, pool], 0))
            bit *= 2
        s2 = national_target / nat.reshape(AGE * SEX, HH * TU)

        m_kz = zlo + ks
        m_valid = m_kz <= zhi
        m_slot = slot_of[jnp.minimum(m_kz, zones - 1)]
        m_grp = m_slot // pool_rows
        m_rank = jnp.sum(((m_grp[:, None] == m_grp[None, :]) & m_valid[None, :] & (ks[None, :] < ks[:, None])).astype(jnp.int32), axis=1)
        mine = c_valid & (c_grp == col)
        dest = jnp.broadcast_to(jnp.arange(cols, dtype=jnp.int32)[:, None], (cols, most))

        def route(room):
            keep = mine & (c_rank < room)
            at = jnp.zeros((cols, room), jnp.int32).at[jnp.where(keep, dest, cols), c_rank].set(c_slot % pool_rows, mode="drop")
            sent = jnp.take(pool, at.reshape(-1), axis=0).reshape(cols, room, width)
            came = lax.all_to_all(sent, "col", 0, 0, tiled=True)
            return came[m_grp, jnp.minimum(m_rank, room - 1)]

        target = lax.cond(flag[0, 0] > 0, lambda: route(most), lambda: route(ROOMY))

        w = s1[:, :, None] * s2[None, :, :]
        am = jnp.sum(view * w[:, :, None, :], axis=3)
        am = jnp.sum(am.reshape(count, AGE, SEX, INC), axis=2).reshape(count, AGE * INC)
        k_a = area_zone - zlo
        onehot = (k_a[:, None] == ks[None, :]).astype(f32)
        zp = jnp.sum(onehot[:, :, None] * am[:, None, :], axis=0)
        nk = zhi - zlo
        right = [(i, i + 1) for i in range(n - 1)]
        left = [(i, i - 1) for i in range(1, n)]
        to_right = jnp.stack([zp[nk], jnp.where(lanes == 0, zhi.astype(f32), -1.0)])
        to_left = jnp.stack([zp[0], jnp.where(lanes == 0, zlo.astype(f32), -1.0)])
        from_left = lax.ppermute(to_right, AXES, right)
        from_right = lax.ppermute(to_left, AXES, left)
        zp = zp.at[0].add(jnp.where((from_left[1, 0] == zlo.astype(f32)) & (idx > 0), from_left[0], 0.0))
        zp = zp.at[nk].add(jnp.where((from_right[1, 0] == zhi.astype(f32)) & (idx < n - 1), from_right[0], 0.0))
        ratio = target / zp
        ratio_a = jnp.take(ratio, k_a, axis=0)

        fac = w.reshape(count, AGE, SEX, 1, HH * TU) * ratio_a.reshape(count, AGE, 1, INC, 1)
        out = population.reshape(count, AGE, SEX, INC, HH * TU) * fac
        return out.reshape(count, AGE * SEX, INC * HH * TU)

    return body


def solution(mesh):
    n = mesh.shape["area"]
    grid = Mesh(np.asarray(mesh.devices).reshape(n // MEMBERS, MEMBERS), AXES)
    placed = (P(AXES, None, None), P(AXES, None), P(), P(AXES, None), P(AXES), P())
    return jax.shard_map(
        make_body(n), mesh=grid, in_specs=placed, out_specs=P(AXES, None, None), check_vma=False
    )
```

```python
import jax
import jax.numpy as jnp
import numpy as np
from jax import lax
from jax.experimental import pallas as pl
from jax.sharding import Mesh, PartitionSpec as P

AGE = 48
SEX = 2
INC = 32
HH = 8
TU = 4
ZONE_MOST = 6
MEMBERS = 8
ROOMY = 5
AXES = ("col", "mem")


HI = lax.Precision.HIGHEST
BLOCK = 2
LANES = (((1,), (1,)), ((), ()))


def _sum_kernel(pop_ref, e1_ref, o_ref):
    for b in range(pop_ref.shape[0]):
        o_ref[b] = lax.dot_general(pop_ref[b], e1_ref[...], LANES, precision=HI, preferred_element_type=jnp.float32)


def _margin_kernel(pop_ref, w_ref, e1_ref, e2_ref, o_ref):
    for b in range(pop_ref.shape[0]):
        wide = jnp.dot(w_ref[b], e1_ref[...], precision=HI, preferred_element_type=jnp.float32)
        o_ref[b] = lax.dot_general(pop_ref[b] * wide, e2_ref[...], LANES, precision=HI, preferred_element_type=jnp.float32)


def _fit_kernel(pop_ref, w_ref, r_ref, e1_ref, e2_ref, o_ref):
    for b in range(pop_ref.shape[0]):
        wide = jnp.dot(w_ref[b], e1_ref[...], precision=HI, preferred_element_type=jnp.float32)
        rep = jnp.dot(r_ref[b], e2_ref[...], precision=HI, preferred_element_type=jnp.float32)
        o_ref[b] = pop_ref[b] * wide * rep


def _table_call(kernel, table, smalls, consts, out_last):
    count, rows, width = table.shape
    grid = (count // BLOCK,)
    specs = [pl.BlockSpec((BLOCK, rows, width), lambda i: (i, 0, 0))]
    specs += [pl.BlockSpec((BLOCK,) + x.shape[1:], lambda i: (i, 0, 0)) for x in smalls]
    specs += [pl.BlockSpec(c.shape, lambda i: (0, 0)) for c in consts]
    return pl.pallas_call(
        kernel,
        grid=grid,
        in_specs=specs,
        out_specs=pl.BlockSpec((BLOCK, rows, out_last), lambda i: (i, 0, 0)),
        out_shape=jax.ShapeDtypeStruct((count, rows, out_last), jnp.float32),
    )(table, *smalls, *consts)


def _xor(x, n, bit):
    return lax.ppermute(x, AXES, [(i, i ^ bit) for i in range(n)])


def make_body(n):
    cols = n // MEMBERS

    def body(population, area_target, national_target, zone_target, area_zone, zone_order):
        count = population.shape[0]
        rows = zone_target.shape[0]
        zones = zone_order.shape[0]
        width = zone_target.shape[1]
        most = count
        pool_rows = rows * MEMBERS
        assert ZONE_MOST < count and (AGE * SEX * HH * TU) % width == 0 and 2 * cols <= width
        f32 = jnp.float32
        idx = lax.axis_index(AXES)
        col, mem = idx // MEMBERS, idx % MEMBERS

        labels = jnp.arange(zones, dtype=jnp.int32)
        slot_of = jnp.zeros((zones,), jnp.int32).at[zone_order].set(labels)
        zlo = area_zone[0]
        zhi = area_zone[count - 1]
        ks = jnp.arange(most, dtype=jnp.int32)
        lanes = jnp.arange(width, dtype=jnp.int32)

        lane = jnp.arange(INC * HH * TU, dtype=jnp.int32)
        e1 = (lane[None, :] % (HH * TU) == jnp.arange(HH * TU, dtype=jnp.int32)[:, None]).astype(f32)
        e2 = (lane[None, :] // (HH * TU) == jnp.arange(INC, dtype=jnp.int32)[:, None]).astype(f32)
        t1 = _table_call(_sum_kernel, population, [], [e1], HH * TU)
        area_sum = jnp.sum(t1, axis=2)
        s1 = area_target / area_sum
        part = jnp.sum(t1 * s1[:, :, None], axis=0)
        nat_rows = (AGE * SEX * HH * TU) // width

        zrow = jnp.where(lanes == 2 * col, zlo.astype(f32), 0.0) + jnp.where(lanes == 2 * col + 1, zhi.astype(f32), 0.0)
        msg = jnp.concatenate([part.reshape(nat_rows, width), zrow[None]], axis=0)
        bit = MEMBERS
        while bit < n:
            msg = msg + _xor(msg, n, bit)
            bit *= 2
        nat = msg[:nat_rows]
        zinfo = msg[nat_rows, : 2 * cols].reshape(cols, 2).astype(jnp.int32)

        c_kz = zinfo[:, 0:1] + ks[None, :]
        c_valid = c_kz <= zinfo[:, 1:2]
        c_slot = slot_of[jnp.minimum(c_kz, zones - 1)]
        c_grp = c_slot // pool_rows
        earlier = (c_grp[:, :, None] == c_grp[:, None, :]) & c_valid[:, None, :] & (ks[None, None, :] < ks[None, :, None])
        c_rank = jnp.sum(earlier.astype(jnp.int32), axis=2)
        over = jnp.any(c_valid & (c_rank >= ROOMY)).astype(f32)

        pool = zone_target
        flag = jnp.where(lanes == 0, over, 0.0)[None]
        bit = 1
        while bit < MEMBERS:
            msg = jnp.concatenate([nat, flag, pool], axis=0)
            got = _xor(msg, n, bit)
            nat = nat + got[:nat_rows]
            flag = flag + got[nat_rows:nat_rows + 1]
            theirs = got[nat_rows + 1:]
            pool = jnp.where((mem & bit) == 0, jnp.concatenate([pool, theirs], 0), jnp.concatenate([theirs, pool], 0))
            bit *= 2
        s2 = national_target / nat.reshape(AGE * SEX, HH * TU)

        m_kz = zlo + ks
        m_valid = m_kz <= zhi
        m_slot = slot_of[jnp.minimum(m_kz, zones - 1)]
        m_grp = m_slot // pool_rows
        m_rank = jnp.sum(((m_grp[:, None] == m_grp[None, :]) & m_valid[None, :] & (ks[None, :] < ks[:, None])).astype(jnp.int32), axis=1)
        mine = c_valid & (c_grp == col)

        def route(room):
            keep = mine & (c_rank < room)
            hit = keep[:, :, None] & (c_rank[:, :, None] == jnp.arange(room, dtype=jnp.int32)[None, None, :])
            at = jnp.sum(jnp.where(hit, (c_slot % pool_rows)[:, :, None], 0), axis=1)
            sent = jnp.take(pool, at.reshape(-1), axis=0).reshape(cols, room, width)
            came = lax.all_to_all(sent, "col", 0, 0, tiled=True)
            return came[m_grp, jnp.minimum(m_rank, room - 1)]

        target = lax.cond(flag[0, 0] > 0, lambda: route(most), lambda: route(ROOMY))

        w = s1[:, :, None] * s2[None, :, :]
        am = _table_call(_margin_kernel, population, [w], [e1, e2], INC)
        am = jnp.sum(am.reshape(count, AGE, SEX, INC), axis=2).reshape(count, AGE * INC)
        k_a = area_zone - zlo
        onehot = (k_a[:, None] == ks[None, :]).astype(f32)
        zp = jnp.sum(onehot[:, :, None] * am[:, None, :], axis=0)
        nk = zhi - zlo
        right = [(i, i + 1) for i in range(n - 1)]
        left = [(i, i - 1) for i in range(1, n)]
        to_right = jnp.stack([zp[nk], jnp.where(lanes == 0, zhi.astype(f32), -1.0)])
        to_left = jnp.stack([zp[0], jnp.where(lanes == 0, zlo.astype(f32), -1.0)])
        from_left = lax.ppermute(to_right, AXES, right)
        from_right = lax.ppermute(to_left, AXES, left)
        zp = zp.at[0].add(jnp.where((from_left[1, 0] == zlo.astype(f32)) & (idx > 0), from_left[0], 0.0))
        zp = zp.at[nk].add(jnp.where((from_right[1, 0] == zhi.astype(f32)) & (idx < n - 1), from_right[0], 0.0))
        ratio = target / zp
        ratio_a = jnp.take(ratio, k_a, axis=0)

        r96 = jnp.repeat(ratio_a.reshape(count, AGE, INC), SEX, axis=1)
        return _table_call(_fit_kernel, population, [w, r96], [e1, e2], INC * HH * TU)

    return body


def solution(mesh):
    n = mesh.shape["area"]
    grid = Mesh(np.asarray(mesh.devices).reshape(n // MEMBERS, MEMBERS), AXES)
    placed = (P(AXES, None, None), P(AXES, None), P(), P(AXES, None), P(AXES), P())
    return jax.shard_map(
        make_body(n), mesh=grid, in_specs=placed, out_specs=P(AXES, None, None), check_vma=False
    )
```

```python
import jax
import jax.numpy as jnp
import numpy as np
from jax import lax
from jax.experimental import pallas as pl
from jax.sharding import Mesh, PartitionSpec as P

AGE = 48
SEX = 2
INC = 32
HH = 8
TU = 4
ZONE_MOST = 6
MEMBERS = 8
ROOMY = 5
AXES = ("col", "mem")


HI = lax.Precision.HIGHEST
BLOCK = 2
LANES = (((1,), (1,)), ((), ()))


def _split3(x):
    bf = jnp.bfloat16
    x1 = x.astype(bf)
    r1 = x - x1.astype(jnp.float32)
    x2 = r1.astype(bf)
    x3 = (r1 - x2.astype(jnp.float32)).astype(bf)
    return x1, x2, x3


def _dot3(x, e, dims):
    out = None
    for part in _split3(x):
        term = lax.dot_general(part, e, dims, preferred_element_type=jnp.float32)
        out = term if out is None else out + term
    return out


ROWS = (((1,), (0,)), ((), ()))


def _sum_kernel(pop_ref, g1_ref, o_ref):
    for b in range(pop_ref.shape[0]):
        x = pop_ref[b]
        folded = x[:, 0:128]
        for j in range(1, x.shape[1] // 128):
            folded = folded + x[:, j * 128:(j + 1) * 128]
        o_ref[b] = _dot3(folded, g1_ref[...], ROWS)


def _margin_kernel(pop_ref, s2t_ref, e2t_ref, o_ref):
    for b in range(pop_ref.shape[0]):
        o_ref[b] = _dot3(pop_ref[b] * s2t_ref[...], e2t_ref[...], ROWS)


def _fit_kernel(pop_ref, s1_ref, r_ref, s2t_ref, e2_ref, o_ref):
    for b in range(pop_ref.shape[0]):
        rep = _dot3(r_ref[b], e2_ref[...], ROWS)
        o_ref[b] = pop_ref[b] * (s1_ref[b] * s2t_ref[...]) * rep


def _table_call(kernel, table, smalls, consts, out_last):
    count, rows, width = table.shape
    grid = (count // BLOCK,)
    specs = [pl.BlockSpec((BLOCK, rows, width), lambda i: (i, 0, 0))]
    specs += [pl.BlockSpec((BLOCK,) + x.shape[1:], lambda i: (i, 0, 0)) for x in smalls]
    specs += [pl.BlockSpec(c.shape, lambda i: (0, 0)) for c in consts]
    return pl.pallas_call(
        kernel,
        grid=grid,
        in_specs=specs,
        out_specs=pl.BlockSpec((BLOCK, rows, out_last), lambda i: (i, 0, 0)),
        out_shape=jax.ShapeDtypeStruct((count, rows, out_last), jnp.float32),
    )(table, *smalls, *consts)


def _xor(x, n, bit):
    return lax.ppermute(x, AXES, [(i, i ^ bit) for i in range(n)])


def make_body(n):
    cols = n // MEMBERS

    def body(population, area_target, national_target, zone_target, area_zone, zone_order):
        count = population.shape[0]
        rows = zone_target.shape[0]
        zones = zone_order.shape[0]
        width = zone_target.shape[1]
        most = count
        pool_rows = rows * MEMBERS
        assert ZONE_MOST < count and (AGE * SEX * HH * TU) % width == 0 and 2 * cols <= width
        f32 = jnp.float32
        idx = lax.axis_index(AXES)
        col, mem = idx // MEMBERS, idx % MEMBERS

        labels = jnp.arange(zones, dtype=jnp.int32)
        slot_of = jnp.zeros((zones,), jnp.int32).at[zone_order].set(labels)
        zlo = area_zone[0]
        zhi = area_zone[count - 1]
        ks = jnp.arange(most, dtype=jnp.int32)
        lanes = jnp.arange(width, dtype=jnp.int32)

        lane = jnp.arange(INC * HH * TU, dtype=jnp.int32)
        bf = jnp.bfloat16
        g1 = (jnp.arange(128, dtype=jnp.int32)[:, None] % (HH * TU) == jnp.arange(HH * TU, dtype=jnp.int32)[None, :]).astype(bf)
        e2 = (lane[None, :] // (HH * TU) == jnp.arange(INC, dtype=jnp.int32)[:, None]).astype(bf)
        e2t = e2.T
        t1 = _table_call(_sum_kernel, population, [], [g1], HH * TU)
        area_sum = jnp.sum(t1, axis=2)
        s1 = area_target / area_sum
        part = jnp.sum(t1 * s1[:, :, None], axis=0)
        nat_rows = (AGE * SEX * HH * TU) // width

        zrow = jnp.where(lanes == 2 * col, zlo.astype(f32), 0.0) + jnp.where(lanes == 2 * col + 1, zhi.astype(f32), 0.0)
        msg = jnp.concatenate([part.reshape(nat_rows, width), zrow[None]], axis=0)
        bit = MEMBERS
        while bit < n:
            msg = msg + _xor(msg, n, bit)
            bit *= 2
        nat = msg[:nat_rows]
        zinfo = msg[nat_rows, : 2 * cols].reshape(cols, 2).astype(jnp.int32)

        c_kz = zinfo[:, 0:1] + ks[None, :]
        c_valid = c_kz <= zinfo[:, 1:2]
        c_slot = slot_of[jnp.minimum(c_kz, zones - 1)]
        c_grp = c_slot // pool_rows
        earlier = (c_grp[:, :, None] == c_grp[:, None, :]) & c_valid[:, None, :] & (ks[None, None, :] < ks[None, :, None])
        c_rank = jnp.sum(earlier.astype(jnp.int32), axis=2)
        over = jnp.any(c_valid & (c_rank >= ROOMY)).astype(f32)

        pool = zone_target
        flag = jnp.where(lanes == 0, over, 0.0)[None]
        bit = 1
        while bit < MEMBERS:
            msg = jnp.concatenate([nat, flag, pool], axis=0)
            got = _xor(msg, n, bit)
            nat = nat + got[:nat_rows]
            flag = flag + got[nat_rows:nat_rows + 1]
            theirs = got[nat_rows + 1:]
            pool = jnp.where((mem & bit) == 0, jnp.concatenate([pool, theirs], 0), jnp.concatenate([theirs, pool], 0))
            bit *= 2
        s2 = national_target / nat.reshape(AGE * SEX, HH * TU)

        m_kz = zlo + ks
        m_valid = m_kz <= zhi
        m_slot = slot_of[jnp.minimum(m_kz, zones - 1)]
        m_grp = m_slot // pool_rows
        m_rank = jnp.sum(((m_grp[:, None] == m_grp[None, :]) & m_valid[None, :] & (ks[None, :] < ks[:, None])).astype(jnp.int32), axis=1)
        mine = c_valid & (c_grp == col)

        def route(room):
            keep = mine & (c_rank < room)
            hit = keep[:, :, None] & (c_rank[:, :, None] == jnp.arange(room, dtype=jnp.int32)[None, None, :])
            at = jnp.sum(jnp.where(hit, (c_slot % pool_rows)[:, :, None], 0), axis=1)
            sent = jnp.take(pool, at.reshape(-1), axis=0).reshape(cols, room, width)
            came = lax.all_to_all(sent, "col", 0, 0, tiled=True)
            return came[m_grp, jnp.minimum(m_rank, room - 1)]

        target = lax.cond(flag[0, 0] > 0, lambda: route(most), lambda: route(ROOMY))

        s2t = jnp.tile(s2, (1, INC))
        am = _table_call(_margin_kernel, population, [], [s2t, e2t], INC) * s1[:, :, None]
        am = jnp.sum(am.reshape(count, AGE, SEX, INC), axis=2).reshape(count, AGE * INC)
        k_a = area_zone - zlo
        onehot = (k_a[:, None] == ks[None, :]).astype(f32)
        zp = jnp.sum(onehot[:, :, None] * am[:, None, :], axis=0)
        nk = zhi - zlo
        right = [(i, i + 1) for i in range(n - 1)]
        left = [(i, i - 1) for i in range(1, n)]
        to_right = jnp.stack([zp[nk], jnp.where(lanes == 0, zhi.astype(f32), -1.0)])
        to_left = jnp.stack([zp[0], jnp.where(lanes == 0, zlo.astype(f32), -1.0)])
        from_left = lax.ppermute(to_right, AXES, right)
        from_right = lax.ppermute(to_left, AXES, left)
        zp = zp.at[0].add(jnp.where((from_left[1, 0] == zlo.astype(f32)) & (idx > 0), from_left[0], 0.0))
        zp = zp.at[nk].add(jnp.where((from_right[1, 0] == zhi.astype(f32)) & (idx < n - 1), from_right[0], 0.0))
        ratio = target / zp
        ratio_a = jnp.take(ratio, k_a, axis=0)

        r96 = jnp.repeat(ratio_a.reshape(count, AGE, INC), SEX, axis=1)
        return _table_call(_fit_kernel, population, [s1[:, :, None], r96], [s2t, e2], INC * HH * TU)

    return body


def solution(mesh):
    n = mesh.shape["area"]
    grid = Mesh(np.asarray(mesh.devices).reshape(n // MEMBERS, MEMBERS), AXES)
    placed = (P(AXES, None, None), P(AXES, None), P(), P(AXES, None), P(AXES), P())
    return jax.shard_map(
        make_body(n), mesh=grid, in_specs=placed, out_specs=P(AXES, None, None), check_vma=False
    )
```

```python
import jax
import jax.numpy as jnp
import numpy as np
from jax import lax
from jax.experimental import pallas as pl
from jax.sharding import Mesh, PartitionSpec as P

AGE = 48
SEX = 2
INC = 32
HH = 8
TU = 4
ZONE_MOST = 6
MEMBERS = 8
ROOMY = 6
AXES = ("col", "mem")


HI = lax.Precision.HIGHEST
BLOCK = 2
LANES = (((1,), (1,)), ((), ()))


def _split3(x):
    bf = jnp.bfloat16
    x1 = x.astype(bf)
    r1 = x - x1.astype(jnp.float32)
    x2 = r1.astype(bf)
    x3 = (r1 - x2.astype(jnp.float32)).astype(bf)
    return x1, x2, x3


def _dot3(x, e, dims):
    out = None
    for part in _split3(x):
        term = lax.dot_general(part, e, dims, preferred_element_type=jnp.float32)
        out = term if out is None else out + term
    return out


ROWS = (((1,), (0,)), ((), ()))


def _sum_kernel(pop_ref, g1_ref, o_ref):
    for b in range(pop_ref.shape[0]):
        x = pop_ref[b]
        folded = x[:, 0:128]
        for j in range(1, x.shape[1] // 128):
            folded = folded + x[:, j * 128:(j + 1) * 128]
        o_ref[b] = _dot3(folded, g1_ref[...], ROWS)


def _margin_kernel(pop_ref, s2t_ref, e2t_ref, o_ref):
    for b in range(pop_ref.shape[0]):
        o_ref[b] = _dot3(pop_ref[b] * s2t_ref[...], e2t_ref[...], ROWS)


def _fit_kernel(pop_ref, s1_ref, r_ref, s2t_ref, e2_ref, o_ref):
    for b in range(pop_ref.shape[0]):
        rep = _dot3(r_ref[b], e2_ref[...], ROWS)
        o_ref[b] = pop_ref[b] * (s1_ref[b] * s2t_ref[...]) * rep


def _table_call(kernel, table, smalls, consts, out_last):
    count, rows, width = table.shape
    grid = (count // BLOCK,)
    specs = [pl.BlockSpec((BLOCK, rows, width), lambda i: (i, 0, 0))]
    specs += [pl.BlockSpec((BLOCK,) + x.shape[1:], lambda i: (i, 0, 0)) for x in smalls]
    specs += [pl.BlockSpec(c.shape, lambda i: (0, 0)) for c in consts]
    return pl.pallas_call(
        kernel,
        grid=grid,
        in_specs=specs,
        out_specs=pl.BlockSpec((BLOCK, rows, out_last), lambda i: (i, 0, 0)),
        out_shape=jax.ShapeDtypeStruct((count, rows, out_last), jnp.float32),
    )(table, *smalls, *consts)


def _xor(x, n, bit):
    return lax.ppermute(x, AXES, [(i, i ^ bit) for i in range(n)])


def make_body(n):
    cols = n // MEMBERS

    def body(population, area_target, national_target, zone_target, area_zone, zone_order):
        count = population.shape[0]
        rows = zone_target.shape[0]
        zones = zone_order.shape[0]
        width = zone_target.shape[1]
        most = count
        pool_rows = rows * MEMBERS
        assert ZONE_MOST < count and (AGE * SEX * HH * TU) % width == 0 and 2 * cols <= width
        f32 = jnp.float32
        idx = lax.axis_index(AXES)
        col, mem = idx // MEMBERS, idx % MEMBERS

        labels = jnp.arange(zones, dtype=jnp.int32)

        def slot_of(z):
            return jnp.sum(jnp.where(zone_order[None, :] == z.reshape(-1)[:, None], labels[None, :], 0), axis=1).reshape(z.shape)

        zlo = area_zone[0]
        zhi = area_zone[count - 1]
        ks = jnp.arange(most, dtype=jnp.int32)
        lanes = jnp.arange(width, dtype=jnp.int32)

        m_kz = zlo + ks
        m_valid = m_kz <= zhi
        m_slot = slot_of(jnp.minimum(m_kz, zones - 1))
        m_mem = (m_slot // rows) % MEMBERS
        m_rank = jnp.sum(((m_mem[:, None] == m_mem[None, :]) & m_valid[None, :] & (ks[None, :] < ks[:, None])).astype(jnp.int32), axis=1)
        over = jnp.any(m_valid & (m_rank >= ROOMY)).astype(f32)

        lane = jnp.arange(INC * HH * TU, dtype=jnp.int32)
        bf = jnp.bfloat16
        g1 = (jnp.arange(128, dtype=jnp.int32)[:, None] % (HH * TU) == jnp.arange(HH * TU, dtype=jnp.int32)[None, :]).astype(bf)
        e2 = (lane[None, :] // (HH * TU) == jnp.arange(INC, dtype=jnp.int32)[:, None]).astype(bf)
        e2t = e2.T
        t1 = _table_call(_sum_kernel, population, [], [g1], HH * TU)
        area_sum = jnp.sum(t1, axis=2)
        s1 = area_target / area_sum
        part = jnp.sum(t1 * s1[:, :, None], axis=0)
        nat_rows = (AGE * SEX * HH * TU) // width

        nat = part.reshape(nat_rows, width)
        flag = jnp.where(lanes == 0, over, 0.0)[None]
        pool = zone_target
        bit = MEMBERS
        while bit < n:
            got = _xor(jnp.concatenate([nat, flag, pool], axis=0), n, bit)
            nat = nat + got[:nat_rows]
            flag = flag + got[nat_rows:nat_rows + 1]
            theirs = got[nat_rows + 1:]
            pool = jnp.where((idx & bit) == 0, jnp.concatenate([pool, theirs], 0), jnp.concatenate([theirs, pool], 0))
            bit *= 2

        zrow = jnp.where(lanes == 2 * mem, zlo.astype(f32), 0.0) + jnp.where(lanes == 2 * mem + 1, zhi.astype(f32), 0.0)
        msg = jnp.concatenate([nat, flag, zrow[None]], axis=0)
        bit = 1
        while bit < MEMBERS:
            msg = msg + _xor(msg, n, bit)
            bit *= 2
        nat = msg[:nat_rows]
        total_over = msg[nat_rows, 0]
        zinfo = msg[nat_rows + 1, : 2 * MEMBERS].reshape(MEMBERS, 2).astype(jnp.int32)
        s2 = national_target / nat.reshape(AGE * SEX, HH * TU)

        c_kz = zinfo[:, 0:1] + ks[None, :]
        c_valid = c_kz <= zinfo[:, 1:2]
        c_slot = slot_of(jnp.minimum(c_kz, zones - 1))
        c_mem = (c_slot // rows) % MEMBERS
        earlier = (c_mem[:, :, None] == c_mem[:, None, :]) & c_valid[:, None, :] & (ks[None, None, :] < ks[None, :, None])
        c_rank = jnp.sum(earlier.astype(jnp.int32), axis=2)
        mine = c_valid & (c_mem == mem)
        c_at = (c_slot // (rows * MEMBERS)) * rows + c_slot % rows

        def route(room):
            hit = (mine & (c_rank < room))[:, :, None] & (c_rank[:, :, None] == jnp.arange(room, dtype=jnp.int32)[None, None, :])
            at = jnp.sum(jnp.where(hit, c_at[:, :, None], 0), axis=1)
            sent = jnp.take(pool, at.reshape(-1), axis=0).reshape(MEMBERS, room, width)
            came = lax.all_to_all(sent, "mem", 0, 0, tiled=True)
            return came[m_mem, jnp.minimum(m_rank, room - 1)]

        target = lax.cond(total_over > 0, lambda: route(most), lambda: route(ROOMY))

        s2t = jnp.tile(s2, (1, INC))
        am = _table_call(_margin_kernel, population, [], [s2t, e2t], INC) * s1[:, :, None]
        am = jnp.sum(am.reshape(count, AGE, SEX, INC), axis=2).reshape(count, AGE * INC)
        k_a = area_zone - zlo
        onehot = (k_a[:, None] == ks[None, :]).astype(f32)
        zp = jnp.sum(onehot[:, :, None] * am[:, None, :], axis=0)
        nk = zhi - zlo
        right = [(i, i + 1) for i in range(n - 1)]
        left = [(i, i - 1) for i in range(1, n)]
        to_right = jnp.stack([zp[nk], jnp.where(lanes == 0, zhi.astype(f32), -1.0)])
        to_left = jnp.stack([zp[0], jnp.where(lanes == 0, zlo.astype(f32), -1.0)])
        from_left = lax.ppermute(to_right, AXES, right)
        from_right = lax.ppermute(to_left, AXES, left)
        zp = zp.at[0].add(jnp.where((from_left[1, 0] == zlo.astype(f32)) & (idx > 0), from_left[0], 0.0))
        zp = zp.at[nk].add(jnp.where((from_right[1, 0] == zhi.astype(f32)) & (idx < n - 1), from_right[0], 0.0))
        ratio = target / zp
        ratio_a = jnp.take(ratio, k_a, axis=0)

        r96 = jnp.repeat(ratio_a.reshape(count, AGE, INC), SEX, axis=1)
        return _table_call(_fit_kernel, population, [s1[:, :, None], r96], [s2t, e2], INC * HH * TU)

    return body


def solution(mesh):
    n = mesh.shape["area"]
    grid = Mesh(np.asarray(mesh.devices).reshape(n // MEMBERS, MEMBERS), AXES)
    placed = (P(AXES, None, None), P(AXES, None), P(), P(AXES, None), P(AXES), P())
    return jax.shard_map(
        make_body(n), mesh=grid, in_specs=placed, out_specs=P(AXES, None, None), check_vma=False
    )
```

```python
import jax
import jax.numpy as jnp
import numpy as np
from jax import lax
from jax.experimental import pallas as pl
from jax.sharding import Mesh, PartitionSpec as P

AGE = 48
SEX = 2
INC = 32
HH = 8
TU = 4
ZONE_MOST = 6
MEMBERS = 8
ROOMY = 6
AXES = ("col", "mem")


HI = lax.Precision.HIGHEST
BLOCK = 4
LANES = (((1,), (1,)), ((), ()))


def _split3(x):
    bf = jnp.bfloat16
    x1 = x.astype(bf)
    r1 = x - x1.astype(jnp.float32)
    x2 = r1.astype(bf)
    x3 = (r1 - x2.astype(jnp.float32)).astype(bf)
    return x1, x2, x3


def _dot3(x, e, dims):
    out = None
    for part in _split3(x):
        term = lax.dot_general(part, e, dims, preferred_element_type=jnp.float32)
        out = term if out is None else out + term
    return out


ROWS = (((1,), (0,)), ((), ()))


def _sum_kernel(pop_ref, g1_ref, o_ref):
    for b in range(pop_ref.shape[0]):
        x = pop_ref[b]
        folded = x[:, 0:128]
        for j in range(1, x.shape[1] // 128):
            folded = folded + x[:, j * 128:(j + 1) * 128]
        o_ref[b] = _dot3(folded, g1_ref[...], ROWS)


def _margin_kernel(pop_ref, s2t_ref, e2t_ref, o_ref):
    for b in range(pop_ref.shape[0]):
        o_ref[b] = _dot3(pop_ref[b] * s2t_ref[...], e2t_ref[...], ROWS)


def _fit_kernel(pop_ref, s1_ref, r_ref, s2t_ref, e2_ref, o_ref):
    for b in range(pop_ref.shape[0]):
        rep = _dot3(r_ref[b], e2_ref[...], ROWS)
        o_ref[b] = pop_ref[b] * (s1_ref[b] * s2t_ref[...]) * rep


def _table_call(kernel, table, smalls, consts, out_last):
    count, rows, width = table.shape
    grid = (count // BLOCK,)
    specs = [pl.BlockSpec((BLOCK, rows, width), lambda i: (i, 0, 0))]
    specs += [pl.BlockSpec((BLOCK,) + x.shape[1:], lambda i: (i, 0, 0)) for x in smalls]
    specs += [pl.BlockSpec(c.shape, lambda i: (0, 0)) for c in consts]
    return pl.pallas_call(
        kernel,
        grid=grid,
        in_specs=specs,
        out_specs=pl.BlockSpec((BLOCK, rows, out_last), lambda i: (i, 0, 0)),
        out_shape=jax.ShapeDtypeStruct((count, rows, out_last), jnp.float32),
    )(table, *smalls, *consts)


def _xor(x, n, bit):
    return lax.ppermute(x, AXES, [(i, i ^ bit) for i in range(n)])


def make_body(n):
    cols = n // MEMBERS

    def body(population, area_target, national_target, zone_target, area_zone, zone_order):
        count = population.shape[0]
        rows = zone_target.shape[0]
        zones = zone_order.shape[0]
        width = zone_target.shape[1]
        most = count
        pool_rows = rows * MEMBERS
        assert ZONE_MOST < count and (AGE * SEX * HH * TU) % width == 0 and 2 * cols <= width
        f32 = jnp.float32
        idx = lax.axis_index(AXES)
        col, mem = idx // MEMBERS, idx % MEMBERS

        labels = jnp.arange(zones, dtype=jnp.int32)

        def slot_of(z):
            return jnp.sum(jnp.where(zone_order[None, :] == z.reshape(-1)[:, None], labels[None, :], 0), axis=1).reshape(z.shape)

        zlo = area_zone[0]
        zhi = area_zone[count - 1]
        ks = jnp.arange(most, dtype=jnp.int32)
        lanes = jnp.arange(width, dtype=jnp.int32)

        m_kz = zlo + ks
        m_valid = m_kz <= zhi
        m_slot = slot_of(jnp.minimum(m_kz, zones - 1))
        m_mem = (m_slot // rows) % MEMBERS
        m_rank = jnp.sum(((m_mem[:, None] == m_mem[None, :]) & m_valid[None, :] & (ks[None, :] < ks[:, None])).astype(jnp.int32), axis=1)
        over = jnp.any(m_valid & (m_rank >= ROOMY)).astype(f32)

        lane = jnp.arange(INC * HH * TU, dtype=jnp.int32)
        bf = jnp.bfloat16
        g1 = (jnp.arange(128, dtype=jnp.int32)[:, None] % (HH * TU) == jnp.arange(HH * TU, dtype=jnp.int32)[None, :]).astype(bf)
        e2 = (lane[None, :] // (HH * TU) == jnp.arange(INC, dtype=jnp.int32)[:, None]).astype(bf)
        e2t = e2.T
        t1 = _table_call(_sum_kernel, population, [], [g1], HH * TU)
        area_sum = jnp.sum(t1, axis=2)
        s1 = area_target / area_sum
        part = jnp.sum(t1 * s1[:, :, None], axis=0)
        nat_rows = (AGE * SEX * HH * TU) // width

        nat = part.reshape(nat_rows, width)
        flag = jnp.where(lanes == 0, over, 0.0)[None]
        pool = zone_target
        bit = MEMBERS
        while bit < n:
            got = _xor(jnp.concatenate([nat, flag, pool], axis=0), n, bit)
            nat = nat + got[:nat_rows]
            flag = flag + got[nat_rows:nat_rows + 1]
            theirs = got[nat_rows + 1:]
            pool = jnp.where((idx & bit) == 0, jnp.concatenate([pool, theirs], 0), jnp.concatenate([theirs, pool], 0))
            bit *= 2

        zrow = jnp.where(lanes == 2 * mem, zlo.astype(f32), 0.0) + jnp.where(lanes == 2 * mem + 1, zhi.astype(f32), 0.0)
        msg = jnp.concatenate([nat, flag, zrow[None]], axis=0)
        bit = 1
        while bit < MEMBERS:
            msg = msg + _xor(msg, n, bit)
            bit *= 2
        nat = msg[:nat_rows]
        total_over = msg[nat_rows, 0]
        zinfo = msg[nat_rows + 1, : 2 * MEMBERS].reshape(MEMBERS, 2).astype(jnp.int32)
        s2 = national_target / nat.reshape(AGE * SEX, HH * TU)

        c_kz = zinfo[:, 0:1] + ks[None, :]
        c_valid = c_kz <= zinfo[:, 1:2]
        c_slot = slot_of(jnp.minimum(c_kz, zones - 1))
        c_mem = (c_slot // rows) % MEMBERS
        earlier = (c_mem[:, :, None] == c_mem[:, None, :]) & c_valid[:, None, :] & (ks[None, None, :] < ks[None, :, None])
        c_rank = jnp.sum(earlier.astype(jnp.int32), axis=2)
        mine = c_valid & (c_mem == mem)
        c_at = (c_slot // (rows * MEMBERS)) * rows + c_slot % rows

        def exchange(room, low):
            rank = c_rank - low
            hit = (mine & (rank >= 0) & (rank < room))[:, :, None] & (rank[:, :, None] == jnp.arange(room, dtype=jnp.int32)[None, None, :])
            at = jnp.sum(jnp.where(hit, c_at[:, :, None], 0), axis=1)
            sent = jnp.take(pool, at.reshape(-1), axis=0).reshape(MEMBERS, room, width)
            return lax.all_to_all(sent, "mem", 0, 0, tiled=True)

        fast = exchange(ROOMY, 0)
        spare = most - ROOMY
        slow = lax.cond(total_over > 0, lambda: exchange(spare, ROOMY), lambda: jnp.zeros((MEMBERS, spare, width), f32))
        target = jnp.where((m_rank < ROOMY)[:, None], fast[m_mem, jnp.minimum(m_rank, ROOMY - 1)],
                           slow[m_mem, jnp.clip(m_rank - ROOMY, 0, spare - 1)])

        s2t = jnp.tile(s2, (1, INC))
        am = _table_call(_margin_kernel, population, [], [s2t, e2t], INC) * s1[:, :, None]
        am = jnp.sum(am.reshape(count, AGE, SEX, INC), axis=2).reshape(count, AGE * INC)
        k_a = area_zone - zlo
        onehot = (k_a[:, None] == ks[None, :]).astype(f32)
        zp = jnp.sum(onehot[:, :, None] * am[:, None, :], axis=0)
        nk = zhi - zlo
        right = [(i, i + 1) for i in range(n - 1)]
        left = [(i, i - 1) for i in range(1, n)]
        to_right = jnp.stack([zp[nk], jnp.where(lanes == 0, zhi.astype(f32), -1.0)])
        to_left = jnp.stack([zp[0], jnp.where(lanes == 0, zlo.astype(f32), -1.0)])
        from_left = lax.ppermute(to_right, AXES, right)
        from_right = lax.ppermute(to_left, AXES, left)
        zp = zp.at[0].add(jnp.where((from_left[1, 0] == zlo.astype(f32)) & (idx > 0), from_left[0], 0.0))
        zp = zp.at[nk].add(jnp.where((from_right[1, 0] == zhi.astype(f32)) & (idx < n - 1), from_right[0], 0.0))
        ratio = target / zp
        ratio_a = jnp.take(ratio, k_a, axis=0)

        r96 = jnp.repeat(ratio_a.reshape(count, AGE, INC), SEX, axis=1)
        return _table_call(_fit_kernel, population, [s1[:, :, None], r96], [s2t, e2], INC * HH * TU)

    return body


def solution(mesh):
    n = mesh.shape["area"]
    grid = Mesh(np.asarray(mesh.devices).reshape(n // MEMBERS, MEMBERS), AXES)
    placed = (P(AXES, None, None), P(AXES, None), P(), P(AXES, None), P(AXES), P())
    return jax.shard_map(
        make_body(n), mesh=grid, in_specs=placed, out_specs=P(AXES, None, None), check_vma=False
    )
```

```python
import jax
import jax.numpy as jnp
import numpy as np
from jax import lax
from jax.experimental import pallas as pl
from jax.sharding import Mesh, PartitionSpec as P

AGE = 48
SEX = 2
INC = 32
HH = 8
TU = 4
ZONE_MOST = 6
MEMBERS = 8
ROOMY = 6
AXES = ("col", "mem")


HI = lax.Precision.HIGHEST
BLOCK = 4
LANES = (((1,), (1,)), ((), ()))


def _split3(x):
    bf = jnp.bfloat16
    x1 = x.astype(bf)
    r1 = x - x1.astype(jnp.float32)
    x2 = r1.astype(bf)
    x3 = (r1 - x2.astype(jnp.float32)).astype(bf)
    return x1, x2, x3


def _dot3(x, e, dims):
    out = None
    for part in _split3(x):
        term = lax.dot_general(part, e, dims, preferred_element_type=jnp.float32)
        out = term if out is None else out + term
    return out


ROWS = (((1,), (0,)), ((), ()))


def _sum_kernel(pop_ref, g1_ref, o_ref):
    for b in range(pop_ref.shape[0]):
        x = pop_ref[b]
        folded = x[:, 0:128]
        for j in range(1, x.shape[1] // 128):
            folded = folded + x[:, j * 128:(j + 1) * 128]
        o_ref[b] = _dot3(folded, g1_ref[...], ROWS)


def _margin_kernel(pop_ref, s2t_ref, e2t_ref, o_ref):
    for b in range(pop_ref.shape[0]):
        o_ref[b] = _dot3(pop_ref[b] * s2t_ref[...], e2t_ref[...], ROWS)


def _fit_kernel(pop_ref, r_ref, s2t_ref, e2_ref, o_ref):
    for b in range(pop_ref.shape[0]):
        rep = _dot3(r_ref[b], e2_ref[...], ROWS)
        o_ref[b] = pop_ref[b] * s2t_ref[...] * rep


def _table_call(kernel, table, smalls, consts, out_last):
    count, rows, width = table.shape
    grid = (count // BLOCK,)
    specs = [pl.BlockSpec((BLOCK, rows, width), lambda i: (i, 0, 0))]
    specs += [pl.BlockSpec((BLOCK,) + x.shape[1:], lambda i: (i, 0, 0)) for x in smalls]
    specs += [pl.BlockSpec(c.shape, lambda i: (0, 0)) for c in consts]
    return pl.pallas_call(
        kernel,
        grid=grid,
        in_specs=specs,
        out_specs=pl.BlockSpec((BLOCK, rows, out_last), lambda i: (i, 0, 0)),
        out_shape=jax.ShapeDtypeStruct((count, rows, out_last), jnp.float32),
    )(table, *smalls, *consts)


def _xor(x, n, bit):
    return lax.ppermute(x, AXES, [(i, i ^ bit) for i in range(n)])


def make_body(n):
    cols = n // MEMBERS

    def body(population, area_target, national_target, zone_target, area_zone, zone_order):
        count = population.shape[0]
        rows = zone_target.shape[0]
        zones = zone_order.shape[0]
        width = zone_target.shape[1]
        most = count
        pool_rows = rows * MEMBERS
        assert ZONE_MOST < count and (AGE * SEX * HH * TU) % width == 0 and 2 * cols <= width
        f32 = jnp.float32
        idx = lax.axis_index(AXES)
        col, mem = idx // MEMBERS, idx % MEMBERS

        labels = jnp.arange(zones, dtype=jnp.int32)

        def slot_of(z):
            return jnp.sum(jnp.where(zone_order[None, :] == z.reshape(-1)[:, None], labels[None, :], 0), axis=1).reshape(z.shape)

        zlo = area_zone[0]
        zhi = area_zone[count - 1]
        ks = jnp.arange(most, dtype=jnp.int32)
        lanes = jnp.arange(width, dtype=jnp.int32)

        m_kz = zlo + ks
        m_valid = m_kz <= zhi
        m_slot = slot_of(jnp.minimum(m_kz, zones - 1))
        m_mem = (m_slot // rows) % MEMBERS
        m_rank = jnp.sum(((m_mem[:, None] == m_mem[None, :]) & m_valid[None, :] & (ks[None, :] < ks[:, None])).astype(jnp.int32), axis=1)
        over = jnp.any(m_valid & (m_rank >= ROOMY)).astype(f32)

        bf = jnp.bfloat16
        g1 = jnp.asarray(np.arange(128)[:, None] % (HH * TU) == np.arange(HH * TU)[None, :], bf)
        e2_np = np.arange(INC * HH * TU)[None, :] // (HH * TU) == np.arange(INC)[:, None]
        e2 = jnp.asarray(e2_np, bf)
        e2t = jnp.asarray(e2_np.T, bf)
        t1 = _table_call(_sum_kernel, population, [], [g1], HH * TU)
        area_sum = jnp.sum(t1, axis=2)
        s1 = area_target / area_sum
        part = jnp.sum(t1 * s1[:, :, None], axis=0)
        nat_rows = (AGE * SEX * HH * TU) // width

        nat = part.reshape(nat_rows, width)
        flag = jnp.where(lanes == 0, over, 0.0)[None]
        pool = zone_target
        bit = MEMBERS
        while bit < n:
            got = _xor(jnp.concatenate([nat, flag, pool], axis=0), n, bit)
            nat = nat + got[:nat_rows]
            flag = flag + got[nat_rows:nat_rows + 1]
            theirs = got[nat_rows + 1:]
            pool = jnp.where((idx & bit) == 0, jnp.concatenate([pool, theirs], 0), jnp.concatenate([theirs, pool], 0))
            bit *= 2

        zrow = jnp.where(lanes == 2 * mem, zlo.astype(f32), 0.0) + jnp.where(lanes == 2 * mem + 1, zhi.astype(f32), 0.0)
        msg = jnp.concatenate([nat, flag, zrow[None]], axis=0)
        bit = 1
        while bit < MEMBERS:
            msg = msg + _xor(msg, n, bit)
            bit *= 2
        nat = msg[:nat_rows]
        total_over = msg[nat_rows, 0]
        zinfo = msg[nat_rows + 1, : 2 * MEMBERS].reshape(MEMBERS, 2).astype(jnp.int32)
        s2 = national_target / nat.reshape(AGE * SEX, HH * TU)

        c_kz = zinfo[:, 0:1] + ks[None, :]
        c_valid = c_kz <= zinfo[:, 1:2]
        c_slot = slot_of(jnp.minimum(c_kz, zones - 1))
        c_mem = (c_slot // rows) % MEMBERS
        earlier = (c_mem[:, :, None] == c_mem[:, None, :]) & c_valid[:, None, :] & (ks[None, None, :] < ks[None, :, None])
        c_rank = jnp.sum(earlier.astype(jnp.int32), axis=2)
        mine = c_valid & (c_mem == mem)
        c_at = (c_slot // (rows * MEMBERS)) * rows + c_slot % rows

        def exchange(room, low):
            rank = c_rank - low
            hit = (mine & (rank >= 0) & (rank < room))[:, :, None] & (rank[:, :, None] == jnp.arange(room, dtype=jnp.int32)[None, None, :])
            at = jnp.sum(jnp.where(hit, c_at[:, :, None], 0), axis=1)
            sent = jnp.take(pool, at.reshape(-1), axis=0).reshape(MEMBERS, room, width)
            return lax.all_to_all(sent, "mem", 0, 0, tiled=True)

        fast = exchange(ROOMY, 0)
        spare = most - ROOMY
        slow = lax.cond(total_over > 0, lambda: exchange(spare, ROOMY), lambda: jnp.zeros((MEMBERS, spare, width), f32))
        target = jnp.where((m_rank < ROOMY)[:, None], fast[m_mem, jnp.minimum(m_rank, ROOMY - 1)],
                           slow[m_mem, jnp.clip(m_rank - ROOMY, 0, spare - 1)])

        s2t = jnp.tile(s2, (1, INC))
        am = _table_call(_margin_kernel, population, [], [s2t, e2t], INC) * s1[:, :, None]
        am = jnp.sum(am.reshape(count, AGE, SEX, INC), axis=2).reshape(count, AGE * INC)
        k_a = area_zone - zlo
        onehot = (k_a[:, None] == ks[None, :]).astype(f32)
        zp = jnp.sum(onehot[:, :, None] * am[:, None, :], axis=0)
        nk = zhi - zlo
        right = [(i, i + 1) for i in range(n - 1)]
        left = [(i, i - 1) for i in range(1, n)]
        to_right = jnp.stack([zp[nk], jnp.where(lanes == 0, zhi.astype(f32), -1.0)])
        to_left = jnp.stack([zp[0], jnp.where(lanes == 0, zlo.astype(f32), -1.0)])
        from_left = lax.ppermute(to_right, AXES, right)
        from_right = lax.ppermute(to_left, AXES, left)
        zp = zp.at[0].add(jnp.where((from_left[1, 0] == zlo.astype(f32)) & (idx > 0), from_left[0], 0.0))
        zp = zp.at[nk].add(jnp.where((from_right[1, 0] == zhi.astype(f32)) & (idx < n - 1), from_right[0], 0.0))
        ratio = target / zp
        ratio_a = jnp.take(ratio, k_a, axis=0)

        r96 = jnp.repeat(ratio_a.reshape(count, AGE, INC), SEX, axis=1) * s1[:, :, None]
        return _table_call(_fit_kernel, population, [r96], [s2t, e2], INC * HH * TU)

    return body


def solution(mesh):
    n = mesh.shape["area"]
    grid = Mesh(np.asarray(mesh.devices).reshape(n // MEMBERS, MEMBERS), AXES)
    placed = (P(AXES, None, None), P(AXES, None), P(), P(AXES, None), P(AXES), P())
    return jax.shard_map(
        make_body(n), mesh=grid, in_specs=placed, out_specs=P(AXES, None, None), check_vma=False
    )
```

```python
import jax
import jax.numpy as jnp
import numpy as np
from jax import lax
from jax.experimental import pallas as pl
from jax.sharding import Mesh, PartitionSpec as P

AGE = 48
SEX = 2
INC = 32
HH = 8
TU = 4
ZONE_MOST = 6
MEMBERS = 8
ROOMY = 6
AXES = ("col", "mem")


HI = lax.Precision.HIGHEST
BLOCK = 4
LANES = (((1,), (1,)), ((), ()))


def _split3(x):
    bf = jnp.bfloat16
    x1 = x.astype(bf)
    r1 = x - x1.astype(jnp.float32)
    x2 = r1.astype(bf)
    x3 = (r1 - x2.astype(jnp.float32)).astype(bf)
    return x1, x2, x3


def _dot3(x, e, dims):
    out = None
    for part in _split3(x):
        term = lax.dot_general(part, e, dims, preferred_element_type=jnp.float32)
        out = term if out is None else out + term
    return out


ROWS = (((1,), (0,)), ((), ()))


def _sum_kernel(pop_ref, g1_ref, o_ref):
    for b in range(pop_ref.shape[0]):
        x = pop_ref[b]
        folded = x[:, 0:128]
        for j in range(1, x.shape[1] // 128):
            folded = folded + x[:, j * 128:(j + 1) * 128]
        o_ref[b] = _dot3(folded, g1_ref[...], ROWS)


def _margin_kernel(pop_ref, s2t_ref, e2t_ref, o_ref):
    for b in range(pop_ref.shape[0]):
        o_ref[b] = _dot3(pop_ref[b] * s2t_ref[...], e2t_ref[...], ROWS)


def _fit_kernel(pop_ref, r_ref, s2t_ref, e2_ref, o_ref):
    for b in range(pop_ref.shape[0]):
        rep = _dot3(r_ref[b], e2_ref[...], ROWS)
        o_ref[b] = pop_ref[b] * s2t_ref[...] * rep


def _table_call(kernel, table, smalls, consts, out_last):
    count, rows, width = table.shape
    grid = (count // BLOCK,)
    specs = [pl.BlockSpec((BLOCK, rows, width), lambda i: (i, 0, 0))]
    specs += [pl.BlockSpec((BLOCK,) + x.shape[1:], lambda i: (i, 0, 0)) for x in smalls]
    specs += [pl.BlockSpec(c.shape, lambda i: (0, 0)) for c in consts]
    return pl.pallas_call(
        kernel,
        grid=grid,
        in_specs=specs,
        out_specs=pl.BlockSpec((BLOCK, rows, out_last), lambda i: (i, 0, 0)),
        out_shape=jax.ShapeDtypeStruct((count, rows, out_last), jnp.float32),
    )(table, *smalls, *consts)


def _partner(i, bit):
    if bit in (4, 16, 64):
        low = bit // 2
        r = (i // low) % 4
        return i + ((3 - r) - r) * low
    return i ^ bit


def _xor(x, n, bit):
    return lax.ppermute(x, AXES, [(i, _partner(i, bit)) for i in range(n)])


def make_body(n):
    cols = n // MEMBERS

    def body(population, area_target, national_target, zone_target, area_zone, zone_order):
        count = population.shape[0]
        rows = zone_target.shape[0]
        zones = zone_order.shape[0]
        width = zone_target.shape[1]
        most = count
        pool_rows = rows * MEMBERS
        assert ZONE_MOST < count and (AGE * SEX * HH * TU) % width == 0 and 2 * cols <= width
        f32 = jnp.float32
        idx = lax.axis_index(AXES)
        col, mem = idx // MEMBERS, idx % MEMBERS

        labels = jnp.arange(zones, dtype=jnp.int32)

        def slot_of(z):
            return jnp.sum(jnp.where(zone_order[None, :] == z.reshape(-1)[:, None], labels[None, :], 0), axis=1).reshape(z.shape)

        zlo = area_zone[0]
        zhi = area_zone[count - 1]
        ks = jnp.arange(most, dtype=jnp.int32)
        lanes = jnp.arange(width, dtype=jnp.int32)

        m_kz = zlo + ks
        m_valid = m_kz <= zhi
        m_slot = slot_of(jnp.minimum(m_kz, zones - 1))
        m_mem = (m_slot // rows) % MEMBERS
        m_rank = jnp.sum(((m_mem[:, None] == m_mem[None, :]) & m_valid[None, :] & (ks[None, :] < ks[:, None])).astype(jnp.int32), axis=1)
        over = jnp.any(m_valid & (m_rank >= ROOMY)).astype(f32)

        bf = jnp.bfloat16
        g1 = jnp.asarray(np.arange(128)[:, None] % (HH * TU) == np.arange(HH * TU)[None, :], bf)
        e2_np = np.arange(INC * HH * TU)[None, :] // (HH * TU) == np.arange(INC)[:, None]
        e2 = jnp.asarray(e2_np, bf)
        e2t = jnp.asarray(e2_np.T, bf)
        t1 = _table_call(_sum_kernel, population, [], [g1], HH * TU)
        area_sum = jnp.sum(t1, axis=2)
        s1 = area_target / area_sum
        part = jnp.sum(t1 * s1[:, :, None], axis=0)
        nat_rows = (AGE * SEX * HH * TU) // width

        nat = part.reshape(nat_rows, width)
        flag = jnp.where(lanes == 0, over, 0.0)[None]
        pool = zone_target
        bit = MEMBERS
        while bit < n:
            got = _xor(jnp.concatenate([nat, flag, pool], axis=0), n, bit)
            nat = nat + got[:nat_rows]
            flag = flag + got[nat_rows:nat_rows + 1]
            theirs = got[nat_rows + 1:]
            pool = jnp.where((idx & bit) == 0, jnp.concatenate([pool, theirs], 0), jnp.concatenate([theirs, pool], 0))
            bit *= 2

        zrow = jnp.where(lanes == 2 * mem, zlo.astype(f32), 0.0) + jnp.where(lanes == 2 * mem + 1, zhi.astype(f32), 0.0)
        msg = jnp.concatenate([nat, flag, zrow[None]], axis=0)
        bit = 1
        while bit < MEMBERS:
            msg = msg + _xor(msg, n, bit)
            bit *= 2
        nat = msg[:nat_rows]
        total_over = msg[nat_rows, 0]
        zinfo = msg[nat_rows + 1, : 2 * MEMBERS].reshape(MEMBERS, 2).astype(jnp.int32)
        s2 = national_target / nat.reshape(AGE * SEX, HH * TU)

        c_kz = zinfo[:, 0:1] + ks[None, :]
        c_valid = c_kz <= zinfo[:, 1:2]
        c_slot = slot_of(jnp.minimum(c_kz, zones - 1))
        c_mem = (c_slot // rows) % MEMBERS
        earlier = (c_mem[:, :, None] == c_mem[:, None, :]) & c_valid[:, None, :] & (ks[None, None, :] < ks[None, :, None])
        c_rank = jnp.sum(earlier.astype(jnp.int32), axis=2)
        mine = c_valid & (c_mem == mem)
        c_at = (c_slot // (rows * MEMBERS)) * rows + c_slot % rows

        def exchange(room, low):
            rank = c_rank - low
            hit = (mine & (rank >= 0) & (rank < room))[:, :, None] & (rank[:, :, None] == jnp.arange(room, dtype=jnp.int32)[None, None, :])
            at = jnp.sum(jnp.where(hit, c_at[:, :, None], 0), axis=1)
            sent = jnp.take(pool, at.reshape(-1), axis=0).reshape(MEMBERS, room, width)
            return lax.all_to_all(sent, "mem", 0, 0, tiled=True)

        fast = exchange(ROOMY, 0)
        spare = most - ROOMY
        slow = lax.cond(total_over > 0, lambda: exchange(spare, ROOMY), lambda: jnp.zeros((MEMBERS, spare, width), f32))
        target = jnp.where((m_rank < ROOMY)[:, None], fast[m_mem, jnp.minimum(m_rank, ROOMY - 1)],
                           slow[m_mem, jnp.clip(m_rank - ROOMY, 0, spare - 1)])

        s2t = jnp.tile(s2, (1, INC))
        am = _table_call(_margin_kernel, population, [], [s2t, e2t], INC) * s1[:, :, None]
        am = jnp.sum(am.reshape(count, AGE, SEX, INC), axis=2).reshape(count, AGE * INC)
        k_a = area_zone - zlo
        onehot = (k_a[:, None] == ks[None, :]).astype(f32)
        zp = jnp.sum(onehot[:, :, None] * am[:, None, :], axis=0)
        nk = zhi - zlo
        right = [(i, i + 1) for i in range(n - 1)]
        left = [(i, i - 1) for i in range(1, n)]
        to_right = jnp.stack([zp[nk], jnp.where(lanes == 0, zhi.astype(f32), -1.0)])
        to_left = jnp.stack([zp[0], jnp.where(lanes == 0, zlo.astype(f32), -1.0)])
        from_left = lax.ppermute(to_right, AXES, right)
        from_right = lax.ppermute(to_left, AXES, left)
        zp = zp.at[0].add(jnp.where((from_left[1, 0] == zlo.astype(f32)) & (idx > 0), from_left[0], 0.0))
        zp = zp.at[nk].add(jnp.where((from_right[1, 0] == zhi.astype(f32)) & (idx < n - 1), from_right[0], 0.0))
        ratio = target / zp
        ratio_a = jnp.take(ratio, k_a, axis=0)

        r96 = jnp.repeat(ratio_a.reshape(count, AGE, INC), SEX, axis=1) * s1[:, :, None]
        return _table_call(_fit_kernel, population, [r96], [s2t, e2], INC * HH * TU)

    return body


def solution(mesh):
    n = mesh.shape["area"]
    grid = Mesh(np.asarray(mesh.devices).reshape(n // MEMBERS, MEMBERS), AXES)
    placed = (P(AXES, None, None), P(AXES, None), P(), P(AXES, None), P(AXES), P())
    return jax.shard_map(
        make_body(n), mesh=grid, in_specs=placed, out_specs=P(AXES, None, None), check_vma=False
    )
```

```python
import jax
import jax.numpy as jnp
import numpy as np
from jax import lax
from jax.experimental import pallas as pl
from jax.sharding import Mesh, PartitionSpec as P

AGE = 48
SEX = 2
INC = 32
HH = 8
TU = 4
ZONE_MOST = 6
MEMBERS = 8
ROOMY = 6
AXES = ("col", "mem")


HI = lax.Precision.HIGHEST
BLOCK = 4
LANES = (((1,), (1,)), ((), ()))


def _split3(x):
    bf = jnp.bfloat16
    x1 = x.astype(bf)
    r1 = x - x1.astype(jnp.float32)
    x2 = r1.astype(bf)
    x3 = (r1 - x2.astype(jnp.float32)).astype(bf)
    return x1, x2, x3


def _dot3(x, e, dims):
    out = None
    for part in _split3(x):
        term = lax.dot_general(part, e, dims, preferred_element_type=jnp.float32)
        out = term if out is None else out + term
    return out


ROWS = (((1,), (0,)), ((), ()))


def _sum_kernel(pop_ref, g1_ref, o_ref):
    for b in range(pop_ref.shape[0]):
        x = pop_ref[b]
        folded = x[:, 0:128]
        for j in range(1, x.shape[1] // 128):
            folded = folded + x[:, j * 128:(j + 1) * 128]
        o_ref[b] = _dot3(folded, g1_ref[...], ROWS)


def _margin_kernel(pop_ref, s2t_ref, e2t_ref, o_ref):
    for b in range(pop_ref.shape[0]):
        o_ref[b] = _dot3(pop_ref[b] * s2t_ref[...], e2t_ref[...], ROWS)


def _fit_kernel(pop_ref, r_ref, s2t_ref, e2_ref, o_ref):
    for b in range(pop_ref.shape[0]):
        rep = _dot3(r_ref[b], e2_ref[...], ROWS)
        o_ref[b] = pop_ref[b] * s2t_ref[...] * rep


def _table_call(kernel, table, smalls, consts, out_last):
    count, rows, width = table.shape
    grid = (count // BLOCK,)
    specs = [pl.BlockSpec((BLOCK, rows, width), lambda i: (i, 0, 0))]
    specs += [pl.BlockSpec((BLOCK,) + x.shape[1:], lambda i: (i, 0, 0)) for x in smalls]
    specs += [pl.BlockSpec(c.shape, lambda i: (0, 0)) for c in consts]
    return pl.pallas_call(
        kernel,
        grid=grid,
        in_specs=specs,
        out_specs=pl.BlockSpec((BLOCK, rows, out_last), lambda i: (i, 0, 0)),
        out_shape=jax.ShapeDtypeStruct((count, rows, out_last), jnp.float32),
    )(table, *smalls, *consts)


def _partner(i, bit):
    if bit in (4, 16, 64):
        low = bit // 2
        r = (i // low) % 4
        return i + ((3 - r) - r) * low
    return i ^ bit


def _xor(x, n, bit):
    return lax.ppermute(x, AXES, [(i, _partner(i, bit)) for i in range(n)])


def make_body(n):
    cols = n // MEMBERS

    def body(population, area_target, national_target, zone_target, area_zone, zone_order):
        count = population.shape[0]
        rows = zone_target.shape[0]
        zones = zone_order.shape[0]
        width = zone_target.shape[1]
        most = count
        pool_rows = rows * MEMBERS
        assert ZONE_MOST < count and (AGE * SEX * HH * TU) % width == 0 and 2 * cols <= width
        f32 = jnp.float32
        idx = lax.axis_index(AXES)
        col, mem = idx // MEMBERS, idx % MEMBERS

        labels = jnp.arange(zones, dtype=jnp.int32)

        def slot_of(z):
            return jnp.sum(jnp.where(zone_order[None, :] == z.reshape(-1)[:, None], labels[None, :], 0), axis=1).reshape(z.shape)

        zlo = area_zone[0]
        zhi = area_zone[count - 1]
        ks = jnp.arange(most, dtype=jnp.int32)
        lanes = jnp.arange(width, dtype=jnp.int32)

        m_kz = zlo + ks
        m_valid = m_kz <= zhi
        m_slot = slot_of(jnp.minimum(m_kz, zones - 1))
        m_mem = (m_slot // rows) % MEMBERS
        m_rank = jnp.sum(((m_mem[:, None] == m_mem[None, :]) & m_valid[None, :] & (ks[None, :] < ks[:, None])).astype(jnp.int32), axis=1)
        over = jnp.any(m_valid & (m_rank >= ROOMY)).astype(f32)

        bf = jnp.bfloat16
        g1 = jnp.asarray(np.arange(128)[:, None] % (HH * TU) == np.arange(HH * TU)[None, :], bf)
        e2_np = np.arange(INC * HH * TU)[None, :] // (HH * TU) == np.arange(INC)[:, None]
        e2 = jnp.asarray(e2_np, bf)
        e2t = jnp.asarray(e2_np.T, bf)
        t1 = _table_call(_sum_kernel, population, [], [g1], HH * TU)
        area_sum = jnp.sum(t1, axis=2)
        s1 = area_target / area_sum
        part = jnp.sum(t1 * s1[:, :, None], axis=0)
        nat_rows = (AGE * SEX * HH * TU) // width

        nat = part.reshape(nat_rows, width)
        flag = jnp.where(lanes == 0, over, 0.0)[None]
        pool = zone_target
        bit = MEMBERS
        while bit < n:
            got = _xor(jnp.concatenate([nat, flag, pool], axis=0), n, bit)
            nat = nat + got[:nat_rows]
            flag = flag + got[nat_rows:nat_rows + 1]
            theirs = got[nat_rows + 1:]
            pool = jnp.where((idx & bit) == 0, jnp.concatenate([pool, theirs], 0), jnp.concatenate([theirs, pool], 0))
            bit *= 2

        zrow = jnp.where(lanes == 2 * mem, zlo.astype(f32), 0.0) + jnp.where(lanes == 2 * mem + 1, zhi.astype(f32), 0.0)
        msg = jnp.concatenate([nat, flag, zrow[None]], axis=0)
        bit = 1
        while bit < MEMBERS:
            msg = msg + _xor(msg, n, bit)
            bit *= 2
        nat = msg[:nat_rows]
        total_over = msg[nat_rows, 0]
        zinfo = msg[nat_rows + 1, : 2 * MEMBERS].reshape(MEMBERS, 2).astype(jnp.int32)
        s2 = national_target / nat.reshape(AGE * SEX, HH * TU)

        c_kz = zinfo[:, 0:1] + ks[None, :]
        c_valid = c_kz <= zinfo[:, 1:2]
        c_slot = slot_of(jnp.minimum(c_kz, zones - 1))
        c_mem = (c_slot // rows) % MEMBERS
        earlier = (c_mem[:, :, None] == c_mem[:, None, :]) & c_valid[:, None, :] & (ks[None, None, :] < ks[None, :, None])
        c_rank = jnp.sum(earlier.astype(jnp.int32), axis=2)
        mine = c_valid & (c_mem == mem)
        c_at = (c_slot // (rows * MEMBERS)) * rows + c_slot % rows

        def exchange(room, low):
            rank = c_rank - low
            hit = (mine & (rank >= 0) & (rank < room))[:, :, None] & (rank[:, :, None] == jnp.arange(room, dtype=jnp.int32)[None, None, :])
            at = jnp.sum(jnp.where(hit, c_at[:, :, None], 0), axis=1)
            sent = jnp.take(pool, at.reshape(-1), axis=0).reshape(MEMBERS, room, width)
            return lax.all_to_all(sent, "mem", 0, 0, tiled=True)

        fast = exchange(ROOMY, 0)
        spare = most - ROOMY
        slow = lax.cond(total_over > 0, lambda: exchange(spare, ROOMY), lambda: jnp.zeros((MEMBERS, spare, width), f32))
        fast, s2 = lax.optimization_barrier((fast, s2))
        target = jnp.where((m_rank < ROOMY)[:, None], fast[m_mem, jnp.minimum(m_rank, ROOMY - 1)],
                           slow[m_mem, jnp.clip(m_rank - ROOMY, 0, spare - 1)])

        s2t = jnp.tile(s2, (1, INC))
        am = _table_call(_margin_kernel, population, [], [s2t, e2t], INC) * s1[:, :, None]
        am = jnp.sum(am.reshape(count, AGE, SEX, INC), axis=2).reshape(count, AGE * INC)
        k_a = area_zone - zlo
        onehot = (k_a[:, None] == ks[None, :]).astype(f32)
        zp = jnp.sum(onehot[:, :, None] * am[:, None, :], axis=0)
        nk = zhi - zlo
        right = [(i, i + 1) for i in range(n - 1)]
        left = [(i, i - 1) for i in range(1, n)]
        to_right = jnp.stack([zp[nk], jnp.where(lanes == 0, zhi.astype(f32), -1.0)])
        to_left = jnp.stack([zp[0], jnp.where(lanes == 0, zlo.astype(f32), -1.0)])
        from_left = lax.ppermute(to_right, AXES, right)
        from_right = lax.ppermute(to_left, AXES, left)
        zp = zp.at[0].add(jnp.where((from_left[1, 0] == zlo.astype(f32)) & (idx > 0), from_left[0], 0.0))
        zp = zp.at[nk].add(jnp.where((from_right[1, 0] == zhi.astype(f32)) & (idx < n - 1), from_right[0], 0.0))
        ratio = target / zp
        ratio_a = jnp.take(ratio, k_a, axis=0)

        r96 = jnp.repeat(ratio_a.reshape(count, AGE, INC), SEX, axis=1) * s1[:, :, None]
        return _table_call(_fit_kernel, population, [r96], [s2t, e2], INC * HH * TU)

    return body


def solution(mesh):
    n = mesh.shape["area"]
    grid = Mesh(np.asarray(mesh.devices).reshape(n // MEMBERS, MEMBERS), AXES)
    placed = (P(AXES, None, None), P(AXES, None), P(), P(AXES, None), P(AXES), P())
    return jax.shard_map(
        make_body(n), mesh=grid, in_specs=placed, out_specs=P(AXES, None, None), check_vma=False
    )
```

```python
import jax
import jax.numpy as jnp
import numpy as np
from jax import lax
from jax.experimental import pallas as pl
from jax.sharding import Mesh, PartitionSpec as P

AGE = 48
SEX = 2
INC = 32
HH = 8
TU = 4
ZONE_MOST = 6
MEMBERS = 8
ROOMY = 6
AXES = ("col", "mem")


HI = lax.Precision.HIGHEST
BLOCK = 4
LANES = (((1,), (1,)), ((), ()))


def _split3(x):
    bf = jnp.bfloat16
    x1 = x.astype(bf)
    r1 = x - x1.astype(jnp.float32)
    x2 = r1.astype(bf)
    x3 = (r1 - x2.astype(jnp.float32)).astype(bf)
    return x1, x2, x3


def _split2(x):
    x1 = x.astype(jnp.bfloat16)
    return x1, (x - x1.astype(jnp.float32)).astype(jnp.bfloat16)


def _dot3(x, e, dims, split=_split3):
    out = None
    for part in split(x):
        term = lax.dot_general(part, e, dims, preferred_element_type=jnp.float32)
        out = term if out is None else out + term
    return out


ROWS = (((1,), (0,)), ((), ()))


def _sum_kernel(pop_ref, g1_ref, o_ref):
    for b in range(pop_ref.shape[0]):
        x = pop_ref[b]
        folded = x[:, 0:128]
        for j in range(1, x.shape[1] // 128):
            folded = folded + x[:, j * 128:(j + 1) * 128]
        o_ref[b] = _dot3(folded, g1_ref[...], ROWS)


def _margin_kernel(pop_ref, s2t_ref, e2t_ref, o_ref):
    for b in range(pop_ref.shape[0]):
        o_ref[b] = _dot3(pop_ref[b] * s2t_ref[...], e2t_ref[...], ROWS, _split2)


def _fit_kernel(pop_ref, r_ref, s2t_ref, e2_ref, o_ref):
    for b in range(pop_ref.shape[0]):
        rep = _dot3(r_ref[b], e2_ref[...], ROWS)
        o_ref[b] = pop_ref[b] * s2t_ref[...] * rep


def _table_call(kernel, table, smalls, consts, out_last):
    count, rows, width = table.shape
    grid = (count // BLOCK,)
    specs = [pl.BlockSpec((BLOCK, rows, width), lambda i: (i, 0, 0))]
    specs += [pl.BlockSpec((BLOCK,) + x.shape[1:], lambda i: (i, 0, 0)) for x in smalls]
    specs += [pl.BlockSpec(c.shape, lambda i: (0, 0)) for c in consts]
    return pl.pallas_call(
        kernel,
        grid=grid,
        in_specs=specs,
        out_specs=pl.BlockSpec((BLOCK, rows, out_last), lambda i: (i, 0, 0)),
        out_shape=jax.ShapeDtypeStruct((count, rows, out_last), jnp.float32),
    )(table, *smalls, *consts)


def _partner(i, bit):
    if bit in (4, 16, 64):
        low = bit // 2
        r = (i // low) % 4
        return i + ((3 - r) - r) * low
    return i ^ bit


def _xor(x, n, bit):
    return lax.ppermute(x, AXES, [(i, _partner(i, bit)) for i in range(n)])


def make_body(n):
    cols = n // MEMBERS

    def body(population, area_target, national_target, zone_target, area_zone, zone_order):
        count = population.shape[0]
        rows = zone_target.shape[0]
        zones = zone_order.shape[0]
        width = zone_target.shape[1]
        most = count
        pool_rows = rows * MEMBERS
        assert ZONE_MOST < count and (AGE * SEX * HH * TU) % width == 0 and 2 * cols <= width
        f32 = jnp.float32
        idx = lax.axis_index(AXES)
        col, mem = idx // MEMBERS, idx % MEMBERS

        labels = jnp.arange(zones, dtype=jnp.int32)

        def slot_of(z):
            return jnp.sum(jnp.where(zone_order[None, :] == z.reshape(-1)[:, None], labels[None, :], 0), axis=1).reshape(z.shape)

        zlo = area_zone[0]
        zhi = area_zone[count - 1]
        ks = jnp.arange(most, dtype=jnp.int32)
        lanes = jnp.arange(width, dtype=jnp.int32)

        m_kz = zlo + ks
        m_valid = m_kz <= zhi
        m_slot = slot_of(jnp.minimum(m_kz, zones - 1))
        m_mem = (m_slot // rows) % MEMBERS
        m_rank = jnp.sum(((m_mem[:, None] == m_mem[None, :]) & m_valid[None, :] & (ks[None, :] < ks[:, None])).astype(jnp.int32), axis=1)
        over = jnp.any(m_valid & (m_rank >= ROOMY)).astype(f32)

        bf = jnp.bfloat16
        g1 = jnp.asarray(np.arange(128)[:, None] % (HH * TU) == np.arange(HH * TU)[None, :], bf)
        e2_np = np.arange(INC * HH * TU)[None, :] // (HH * TU) == np.arange(INC)[:, None]
        e2 = jnp.asarray(e2_np, bf)
        e2t = jnp.asarray(e2_np.T, bf)
        t1 = _table_call(_sum_kernel, population, [], [g1], HH * TU)
        area_sum = jnp.sum(t1, axis=2)
        s1 = area_target / area_sum
        part = jnp.sum(t1 * s1[:, :, None], axis=0)
        nat_rows = (AGE * SEX * HH * TU) // width

        nat = part.reshape(nat_rows, width)
        flag = jnp.where(lanes == 0, over, 0.0)[None]
        pool = zone_target
        bit = MEMBERS
        while bit < n:
            got = _xor(jnp.concatenate([nat, flag, pool], axis=0), n, bit)
            nat = nat + got[:nat_rows]
            flag = flag + got[nat_rows:nat_rows + 1]
            theirs = got[nat_rows + 1:]
            pool = jnp.where((idx & bit) == 0, jnp.concatenate([pool, theirs], 0), jnp.concatenate([theirs, pool], 0))
            bit *= 2

        zrow = jnp.where(lanes == 2 * mem, zlo.astype(f32), 0.0) + jnp.where(lanes == 2 * mem + 1, zhi.astype(f32), 0.0)
        msg = jnp.concatenate([nat, flag, zrow[None]], axis=0)
        bit = 1
        while bit < MEMBERS:
            msg = msg + _xor(msg, n, bit)
            bit *= 2
        nat = msg[:nat_rows]
        total_over = msg[nat_rows, 0]
        zinfo = msg[nat_rows + 1, : 2 * MEMBERS].reshape(MEMBERS, 2).astype(jnp.int32)
        s2 = national_target / nat.reshape(AGE * SEX, HH * TU)

        c_kz = zinfo[:, 0:1] + ks[None, :]
        c_valid = c_kz <= zinfo[:, 1:2]
        c_slot = slot_of(jnp.minimum(c_kz, zones - 1))
        c_mem = (c_slot // rows) % MEMBERS
        earlier = (c_mem[:, :, None] == c_mem[:, None, :]) & c_valid[:, None, :] & (ks[None, None, :] < ks[None, :, None])
        c_rank = jnp.sum(earlier.astype(jnp.int32), axis=2)
        mine = c_valid & (c_mem == mem)
        c_at = (c_slot // (rows * MEMBERS)) * rows + c_slot % rows

        def exchange(room, low):
            rank = c_rank - low
            hit = (mine & (rank >= 0) & (rank < room))[:, :, None] & (rank[:, :, None] == jnp.arange(room, dtype=jnp.int32)[None, None, :])
            at = jnp.sum(jnp.where(hit, c_at[:, :, None], 0), axis=1)
            sent = jnp.take(pool, at.reshape(-1), axis=0).reshape(MEMBERS, room, width)
            return lax.all_to_all(sent, "mem", 0, 0, tiled=True)

        fast = exchange(ROOMY, 0)
        spare = most - ROOMY
        slow = lax.cond(total_over > 0, lambda: exchange(spare, ROOMY), lambda: jnp.zeros((MEMBERS, spare, width), f32))
        target = jnp.where((m_rank < ROOMY)[:, None], fast[m_mem, jnp.minimum(m_rank, ROOMY - 1)],
                           slow[m_mem, jnp.clip(m_rank - ROOMY, 0, spare - 1)])

        s2t = jnp.tile(s2, (1, INC))
        am = _table_call(_margin_kernel, population, [], [s2t, e2t], INC) * s1[:, :, None]
        am = jnp.sum(am.reshape(count, AGE, SEX, INC), axis=2).reshape(count, AGE * INC)
        k_a = area_zone - zlo
        onehot = (k_a[:, None] == ks[None, :]).astype(f32)
        zp = jnp.sum(onehot[:, :, None] * am[:, None, :], axis=0)
        nk = zhi - zlo
        right = [(i, i + 1) for i in range(n - 1)]
        left = [(i, i - 1) for i in range(1, n)]
        to_right = jnp.stack([zp[nk], jnp.where(lanes == 0, zhi.astype(f32), -1.0)])
        to_left = jnp.stack([zp[0], jnp.where(lanes == 0, zlo.astype(f32), -1.0)])
        from_left = lax.ppermute(to_right, AXES, right)
        from_right = lax.ppermute(to_left, AXES, left)
        zp = zp.at[0].add(jnp.where((from_left[1, 0] == zlo.astype(f32)) & (idx > 0), from_left[0], 0.0))
        zp = zp.at[nk].add(jnp.where((from_right[1, 0] == zhi.astype(f32)) & (idx < n - 1), from_right[0], 0.0))
        ratio = target / zp
        ratio_a = jnp.take(ratio, k_a, axis=0)

        r96 = jnp.repeat(ratio_a.reshape(count, AGE, INC), SEX, axis=1) * s1[:, :, None]
        return _table_call(_fit_kernel, population, [r96], [s2t, e2], INC * HH * TU)

    return body


def solution(mesh):
    n = mesh.shape["area"]
    grid = Mesh(np.asarray(mesh.devices).reshape(n // MEMBERS, MEMBERS), AXES)
    placed = (P(AXES, None, None), P(AXES, None), P(), P(AXES, None), P(AXES), P())
    return jax.shard_map(
        make_body(n), mesh=grid, in_specs=placed, out_specs=P(AXES, None, None), check_vma=False
    )
```

```python
import jax
import jax.numpy as jnp
import numpy as np
from jax import lax
from jax.experimental import pallas as pl
from jax.sharding import Mesh, PartitionSpec as P

AGE = 48
SEX = 2
INC = 32
HH = 8
TU = 4
ZONE_MOST = 6
MEMBERS = 8
ROOMY = 6
AXES = ("col", "mem")
SHIP_APART = 32


HI = lax.Precision.HIGHEST
BLOCK = 4
LANES = (((1,), (1,)), ((), ()))


def _split3(x):
    bf = jnp.bfloat16
    x1 = x.astype(bf)
    r1 = x - x1.astype(jnp.float32)
    x2 = r1.astype(bf)
    x3 = (r1 - x2.astype(jnp.float32)).astype(bf)
    return x1, x2, x3


def _dot3(x, e, dims):
    out = None
    for part in _split3(x):
        term = lax.dot_general(part, e, dims, preferred_element_type=jnp.float32)
        out = term if out is None else out + term
    return out


ROWS = (((1,), (0,)), ((), ()))


def _sum_kernel(pop_ref, g1_ref, o_ref):
    for b in range(pop_ref.shape[0]):
        x = pop_ref[b]
        folded = x[:, 0:128]
        for j in range(1, x.shape[1] // 128):
            folded = folded + x[:, j * 128:(j + 1) * 128]
        o_ref[b] = _dot3(folded, g1_ref[...], ROWS)


def _margin_kernel(pop_ref, s2t_ref, e2t_ref, o_ref):
    for b in range(pop_ref.shape[0]):
        o_ref[b] = _dot3(pop_ref[b] * s2t_ref[...], e2t_ref[...], ROWS)


def _fit_kernel(pop_ref, r_ref, s2t_ref, e2_ref, o_ref):
    for b in range(pop_ref.shape[0]):
        rep = _dot3(r_ref[b], e2_ref[...], ROWS)
        o_ref[b] = pop_ref[b] * s2t_ref[...] * rep


def _table_call(kernel, table, smalls, consts, out_last):
    count, rows, width = table.shape
    grid = (count // BLOCK,)
    specs = [pl.BlockSpec((BLOCK, rows, width), lambda i: (i, 0, 0))]
    specs += [pl.BlockSpec((BLOCK,) + x.shape[1:], lambda i: (i, 0, 0)) for x in smalls]
    specs += [pl.BlockSpec(c.shape, lambda i: (0, 0)) for c in consts]
    return pl.pallas_call(
        kernel,
        grid=grid,
        in_specs=specs,
        out_specs=pl.BlockSpec((BLOCK, rows, out_last), lambda i: (i, 0, 0)),
        out_shape=jax.ShapeDtypeStruct((count, rows, out_last), jnp.float32),
    )(table, *smalls, *consts)


def _partner(i, bit):
    if bit in (4, 16, 64):
        low = bit // 2
        r = (i // low) % 4
        return i + ((3 - r) - r) * low
    return i ^ bit


def _xor(x, n, bit):
    return lax.ppermute(x, AXES, [(i, _partner(i, bit)) for i in range(n)])


def make_body(n):
    cols = n // MEMBERS

    def body(population, area_target, national_target, zone_target, area_zone, zone_order):
        count = population.shape[0]
        rows = zone_target.shape[0]
        zones = zone_order.shape[0]
        width = zone_target.shape[1]
        most = count
        pool_rows = rows * MEMBERS
        assert ZONE_MOST < count and (AGE * SEX * HH * TU) % width == 0 and 2 * cols <= width
        f32 = jnp.float32
        idx = lax.axis_index(AXES)
        col, mem = idx // MEMBERS, idx % MEMBERS

        labels = jnp.arange(zones, dtype=jnp.int32)

        def slot_of(z):
            return jnp.sum(jnp.where(zone_order[None, :] == z.reshape(-1)[:, None], labels[None, :], 0), axis=1).reshape(z.shape)

        zlo = area_zone[0]
        zhi = area_zone[count - 1]
        ks = jnp.arange(most, dtype=jnp.int32)
        lanes = jnp.arange(width, dtype=jnp.int32)

        m_kz = zlo + ks
        m_valid = m_kz <= zhi
        m_slot = slot_of(jnp.minimum(m_kz, zones - 1))
        m_mem = (m_slot // rows) % MEMBERS
        m_rank = jnp.sum(((m_mem[:, None] == m_mem[None, :]) & m_valid[None, :] & (ks[None, :] < ks[:, None])).astype(jnp.int32), axis=1)
        over = jnp.any(m_valid & (m_rank >= ROOMY)).astype(f32)

        bf = jnp.bfloat16
        g1 = jnp.asarray(np.arange(128)[:, None] % (HH * TU) == np.arange(HH * TU)[None, :], bf)
        e2_np = np.arange(INC * HH * TU)[None, :] // (HH * TU) == np.arange(INC)[:, None]
        e2 = jnp.asarray(e2_np, bf)
        e2t = jnp.asarray(e2_np.T, bf)
        t1 = _table_call(_sum_kernel, population, [], [g1], HH * TU)
        area_sum = jnp.sum(t1, axis=2)
        s1 = area_target / area_sum
        part = jnp.sum(t1 * s1[:, :, None], axis=0)
        nat_rows = (AGE * SEX * HH * TU) // width

        nat = part.reshape(nat_rows, width)
        flag = jnp.where(lanes == 0, over, 0.0)[None]
        pool = zone_target
        bit = MEMBERS
        while bit < n:
            if pool.shape[0] < SHIP_APART:
                got = _xor(jnp.concatenate([nat, flag, pool], axis=0), n, bit)
                theirs = got[nat_rows + 1:]
            else:
                got = _xor(jnp.concatenate([nat, flag], axis=0), n, bit)
                theirs = _xor(pool, n, bit)
            nat = nat + got[:nat_rows]
            flag = flag + got[nat_rows:nat_rows + 1]
            pool = jnp.where((idx & bit) == 0, jnp.concatenate([pool, theirs], 0), jnp.concatenate([theirs, pool], 0))
            bit *= 2

        zrow = jnp.where(lanes == 2 * mem, zlo.astype(f32), 0.0) + jnp.where(lanes == 2 * mem + 1, zhi.astype(f32), 0.0)
        msg = jnp.concatenate([nat, flag, zrow[None]], axis=0)
        bit = 1
        while bit < MEMBERS:
            msg = msg + _xor(msg, n, bit)
            bit *= 2
        nat = msg[:nat_rows]
        total_over = msg[nat_rows, 0]
        zinfo = msg[nat_rows + 1, : 2 * MEMBERS].reshape(MEMBERS, 2).astype(jnp.int32)
        s2 = national_target / nat.reshape(AGE * SEX, HH * TU)

        c_kz = zinfo[:, 0:1] + ks[None, :]
        c_valid = c_kz <= zinfo[:, 1:2]
        c_slot = slot_of(jnp.minimum(c_kz, zones - 1))
        c_mem = (c_slot // rows) % MEMBERS
        earlier = (c_mem[:, :, None] == c_mem[:, None, :]) & c_valid[:, None, :] & (ks[None, None, :] < ks[None, :, None])
        c_rank = jnp.sum(earlier.astype(jnp.int32), axis=2)
        mine = c_valid & (c_mem == mem)
        c_at = (c_slot // (rows * MEMBERS)) * rows + c_slot % rows

        def exchange(room, low):
            rank = c_rank - low
            hit = (mine & (rank >= 0) & (rank < room))[:, :, None] & (rank[:, :, None] == jnp.arange(room, dtype=jnp.int32)[None, None, :])
            at = jnp.sum(jnp.where(hit, c_at[:, :, None], 0), axis=1)
            sent = jnp.take(pool, at.reshape(-1), axis=0).reshape(MEMBERS, room, width)
            return lax.all_to_all(sent, "mem", 0, 0, tiled=True)

        fast = exchange(ROOMY, 0)
        spare = most - ROOMY
        slow = lax.cond(total_over > 0, lambda: exchange(spare, ROOMY), lambda: jnp.zeros((MEMBERS, spare, width), f32))
        target = jnp.where((m_rank < ROOMY)[:, None], fast[m_mem, jnp.minimum(m_rank, ROOMY - 1)],
                           slow[m_mem, jnp.clip(m_rank - ROOMY, 0, spare - 1)])

        s2t = jnp.tile(s2, (1, INC))
        am = _table_call(_margin_kernel, population, [], [s2t, e2t], INC) * s1[:, :, None]
        am = jnp.sum(am.reshape(count, AGE, SEX, INC), axis=2).reshape(count, AGE * INC)
        k_a = area_zone - zlo
        onehot = (k_a[:, None] == ks[None, :]).astype(f32)
        zp = jnp.sum(onehot[:, :, None] * am[:, None, :], axis=0)
        nk = zhi - zlo
        right = [(i, i + 1) for i in range(n - 1)]
        left = [(i, i - 1) for i in range(1, n)]
        to_right = jnp.stack([zp[nk], jnp.where(lanes == 0, zhi.astype(f32), -1.0)])
        to_left = jnp.stack([zp[0], jnp.where(lanes == 0, zlo.astype(f32), -1.0)])
        from_left = lax.ppermute(to_right, AXES, right)
        from_right = lax.ppermute(to_left, AXES, left)
        zp = zp.at[0].add(jnp.where((from_left[1, 0] == zlo.astype(f32)) & (idx > 0), from_left[0], 0.0))
        zp = zp.at[nk].add(jnp.where((from_right[1, 0] == zhi.astype(f32)) & (idx < n - 1), from_right[0], 0.0))
        ratio = target / zp
        ratio_a = jnp.take(ratio, k_a, axis=0)

        r96 = jnp.repeat(ratio_a.reshape(count, AGE, INC), SEX, axis=1) * s1[:, :, None]
        return _table_call(_fit_kernel, population, [r96], [s2t, e2], INC * HH * TU)

    return body


def solution(mesh):
    n = mesh.shape["area"]
    grid = Mesh(np.asarray(mesh.devices).reshape(n // MEMBERS, MEMBERS), AXES)
    placed = (P(AXES, None, None), P(AXES, None), P(), P(AXES, None), P(AXES), P())
    return jax.shard_map(
        make_body(n), mesh=grid, in_specs=placed, out_specs=P(AXES, None, None), check_vma=False
    )
```

```python
import jax
import jax.numpy as jnp
import numpy as np
from jax import lax
from jax.experimental import pallas as pl
from jax.sharding import Mesh, PartitionSpec as P

AGE = 48
SEX = 2
INC = 32
HH = 8
TU = 4
ZONE_MOST = 6
MEMBERS = 8
ROOMY = 6
AXES = ("col", "mem")
SHIP_APART = 32


HI = lax.Precision.HIGHEST
BLOCK = 4
LANES = (((1,), (1,)), ((), ()))


def _split3(x):
    bf = jnp.bfloat16
    x1 = x.astype(bf)
    r1 = x - x1.astype(jnp.float32)
    x2 = r1.astype(bf)
    x3 = (r1 - x2.astype(jnp.float32)).astype(bf)
    return x1, x2, x3


def _dot3(x, e, dims):
    out = None
    for part in _split3(x):
        term = lax.dot_general(part, e, dims, preferred_element_type=jnp.float32)
        out = term if out is None else out + term
    return out


ROWS = (((1,), (0,)), ((), ()))


def _sum_kernel(pop_ref, g1_ref, o_ref):
    for b in range(pop_ref.shape[0]):
        x = pop_ref[b]
        folded = x[:, 0:128]
        for j in range(1, x.shape[1] // 128):
            folded = folded + x[:, j * 128:(j + 1) * 128]
        o_ref[b] = _dot3(folded, g1_ref[...], ROWS)


def _margin_kernel(pop_ref, s2t_ref, e2t_ref, o_ref):
    for b in range(pop_ref.shape[0]):
        o_ref[b] = _dot3(pop_ref[b] * s2t_ref[...], e2t_ref[...], ROWS)


def _fit_kernel(pop_ref, r_ref, s2t_ref, e2_ref, o_ref):
    for b in range(pop_ref.shape[0]):
        rep = _dot3(r_ref[b], e2_ref[...], ROWS)
        o_ref[b] = pop_ref[b] * s2t_ref[...] * rep


def _table_call(kernel, table, smalls, consts, out_last):
    count, rows, width = table.shape
    grid = (count // BLOCK,)
    specs = [pl.BlockSpec((BLOCK, rows, width), lambda i: (i, 0, 0))]
    specs += [pl.BlockSpec((BLOCK,) + x.shape[1:], lambda i: (i, 0, 0)) for x in smalls]
    specs += [pl.BlockSpec(c.shape, lambda i: (0, 0)) for c in consts]
    return pl.pallas_call(
        kernel,
        grid=grid,
        in_specs=specs,
        out_specs=pl.BlockSpec((BLOCK, rows, out_last), lambda i: (i, 0, 0)),
        out_shape=jax.ShapeDtypeStruct((count, rows, out_last), jnp.float32),
    )(table, *smalls, *consts)


def _partner(i, bit):
    if bit in (4, 16, 64):
        low = bit // 2
        r = (i // low) % 4
        return i + ((3 - r) - r) * low
    return i ^ bit


def _xor(x, n, bit):
    return lax.ppermute(x, AXES, [(i, _partner(i, bit)) for i in range(n)])


def _col_partner(i, k):
    low = MEMBERS << (2 * (k // 2))
    flip_low = (k % 2 == 0) == (i % 2 == 0)
    return i ^ low if flip_low else _partner(i, 2 * low)


def _col_partner_traced(i, k):
    low = MEMBERS << (2 * (k // 2))
    r = (i // low) % 4
    flip_low = (k % 2 == 0) == (i % 2 == 0)
    return jnp.where(flip_low, i ^ low, i + ((3 - r) - r) * low)


def _col_round(x, n, k):
    return lax.ppermute(x, AXES, [(i, _col_partner(i, k)) for i in range(n)])


def make_body(n):
    cols = n // MEMBERS

    def body(population, area_target, national_target, zone_target, area_zone, zone_order):
        count = population.shape[0]
        rows = zone_target.shape[0]
        zones = zone_order.shape[0]
        width = zone_target.shape[1]
        most = count
        pool_rows = rows * MEMBERS
        assert ZONE_MOST < count and (AGE * SEX * HH * TU) % width == 0 and 2 * cols <= width
        f32 = jnp.float32
        idx = lax.axis_index(AXES)
        col, mem = idx // MEMBERS, idx % MEMBERS

        labels = jnp.arange(zones, dtype=jnp.int32)

        def slot_of(z):
            return jnp.sum(jnp.where(zone_order[None, :] == z.reshape(-1)[:, None], labels[None, :], 0), axis=1).reshape(z.shape)

        zlo = area_zone[0]
        zhi = area_zone[count - 1]
        ks = jnp.arange(most, dtype=jnp.int32)
        lanes = jnp.arange(width, dtype=jnp.int32)

        m_kz = zlo + ks
        m_valid = m_kz <= zhi
        m_slot = slot_of(jnp.minimum(m_kz, zones - 1))
        m_mem = (m_slot // rows) % MEMBERS
        m_rank = jnp.sum(((m_mem[:, None] == m_mem[None, :]) & m_valid[None, :] & (ks[None, :] < ks[:, None])).astype(jnp.int32), axis=1)
        over = jnp.any(m_valid & (m_rank >= ROOMY)).astype(f32)

        bf = jnp.bfloat16
        g1 = jnp.asarray(np.arange(128)[:, None] % (HH * TU) == np.arange(HH * TU)[None, :], bf)
        e2_np = np.arange(INC * HH * TU)[None, :] // (HH * TU) == np.arange(INC)[:, None]
        e2 = jnp.asarray(e2_np, bf)
        e2t = jnp.asarray(e2_np.T, bf)
        t1 = _table_call(_sum_kernel, population, [], [g1], HH * TU)
        area_sum = jnp.sum(t1, axis=2)
        s1 = area_target / area_sum
        part = jnp.sum(t1 * s1[:, :, None], axis=0)
        nat_rows = (AGE * SEX * HH * TU) // width

        nat = part.reshape(nat_rows, width)
        flag = jnp.where(lanes == 0, over, 0.0)[None]
        pool = zone_target
        rounds = (cols - 1).bit_length()
        for k in range(rounds):
            if pool.shape[0] < SHIP_APART:
                got = _col_round(jnp.concatenate([nat, flag, pool], axis=0), n, k)
                theirs = got[nat_rows + 1:]
            else:
                got = _col_round(jnp.concatenate([nat, flag], axis=0), n, k)
                theirs = _col_round(pool, n, k)
            nat = nat + got[:nat_rows]
            flag = flag + got[nat_rows:nat_rows + 1]
            pool = jnp.concatenate([pool, theirs], 0)

        def order(i, k):
            if k == 0:
                return [i]
            return order(i, k - 1) + order(_col_partner_traced(i, k - 1), k - 1)

        block_col = jnp.stack(order(idx, rounds)) // MEMBERS
        col_block = jnp.sum(jnp.where(block_col[None, :] == jnp.arange(cols, dtype=jnp.int32)[:, None],
                                      jnp.arange(cols, dtype=jnp.int32)[None, :], 0), axis=1)

        zrow = jnp.where(lanes == 2 * mem, zlo.astype(f32), 0.0) + jnp.where(lanes == 2 * mem + 1, zhi.astype(f32), 0.0)
        msg = jnp.concatenate([nat, flag, zrow[None]], axis=0)
        bit = 1
        while bit < MEMBERS:
            msg = msg + _xor(msg, n, bit)
            bit *= 2
        nat = msg[:nat_rows]
        total_over = msg[nat_rows, 0]
        zinfo = msg[nat_rows + 1, : 2 * MEMBERS].reshape(MEMBERS, 2).astype(jnp.int32)
        s2 = national_target / nat.reshape(AGE * SEX, HH * TU)

        c_kz = zinfo[:, 0:1] + ks[None, :]
        c_valid = c_kz <= zinfo[:, 1:2]
        c_slot = slot_of(jnp.minimum(c_kz, zones - 1))
        c_mem = (c_slot // rows) % MEMBERS
        earlier = (c_mem[:, :, None] == c_mem[:, None, :]) & c_valid[:, None, :] & (ks[None, None, :] < ks[None, :, None])
        c_rank = jnp.sum(earlier.astype(jnp.int32), axis=2)
        mine = c_valid & (c_mem == mem)
        c_at = col_block[c_slot // (rows * MEMBERS)] * rows + c_slot % rows

        def exchange(room, low):
            rank = c_rank - low
            hit = (mine & (rank >= 0) & (rank < room))[:, :, None] & (rank[:, :, None] == jnp.arange(room, dtype=jnp.int32)[None, None, :])
            at = jnp.sum(jnp.where(hit, c_at[:, :, None], 0), axis=1)
            sent = jnp.take(pool, at.reshape(-1), axis=0).reshape(MEMBERS, room, width)
            return lax.all_to_all(sent, "mem", 0, 0, tiled=True)

        fast = exchange(ROOMY, 0)
        spare = most - ROOMY
        slow = lax.cond(total_over > 0, lambda: exchange(spare, ROOMY), lambda: jnp.zeros((MEMBERS, spare, width), f32))
        target = jnp.where((m_rank < ROOMY)[:, None], fast[m_mem, jnp.minimum(m_rank, ROOMY - 1)],
                           slow[m_mem, jnp.clip(m_rank - ROOMY, 0, spare - 1)])

        s2t = jnp.tile(s2, (1, INC))
        am = _table_call(_margin_kernel, population, [], [s2t, e2t], INC) * s1[:, :, None]
        am = jnp.sum(am.reshape(count, AGE, SEX, INC), axis=2).reshape(count, AGE * INC)
        k_a = area_zone - zlo
        onehot = (k_a[:, None] == ks[None, :]).astype(f32)
        zp = jnp.sum(onehot[:, :, None] * am[:, None, :], axis=0)
        nk = zhi - zlo
        right = [(i, i + 1) for i in range(n - 1)]
        left = [(i, i - 1) for i in range(1, n)]
        to_right = jnp.stack([zp[nk], jnp.where(lanes == 0, zhi.astype(f32), -1.0)])
        to_left = jnp.stack([zp[0], jnp.where(lanes == 0, zlo.astype(f32), -1.0)])
        from_left = lax.ppermute(to_right, AXES, right)
        from_right = lax.ppermute(to_left, AXES, left)
        zp = zp.at[0].add(jnp.where((from_left[1, 0] == zlo.astype(f32)) & (idx > 0), from_left[0], 0.0))
        zp = zp.at[nk].add(jnp.where((from_right[1, 0] == zhi.astype(f32)) & (idx < n - 1), from_right[0], 0.0))
        ratio = target / zp
        ratio_a = jnp.take(ratio, k_a, axis=0)

        r96 = jnp.repeat(ratio_a.reshape(count, AGE, INC), SEX, axis=1) * s1[:, :, None]
        return _table_call(_fit_kernel, population, [r96], [s2t, e2], INC * HH * TU)

    return body


def solution(mesh):
    n = mesh.shape["area"]
    grid = Mesh(np.asarray(mesh.devices).reshape(n // MEMBERS, MEMBERS), AXES)
    placed = (P(AXES, None, None), P(AXES, None), P(), P(AXES, None), P(AXES), P())
    return jax.shard_map(
        make_body(n), mesh=grid, in_specs=placed, out_specs=P(AXES, None, None), check_vma=False
    )
```

```python
import jax
import jax.numpy as jnp
import numpy as np
from jax import lax
from jax.experimental import pallas as pl
from jax.sharding import Mesh, PartitionSpec as P

AGE = 48
SEX = 2
INC = 32
HH = 8
TU = 4
ZONE_MOST = 6
MEMBERS = 8
ROOMY = 6
AXES = ("col", "mem")
SHIP_APART = 16


HI = lax.Precision.HIGHEST
BLOCK = 4
LANES = (((1,), (1,)), ((), ()))


def _split3(x):
    bf = jnp.bfloat16
    x1 = x.astype(bf)
    r1 = x - x1.astype(jnp.float32)
    x2 = r1.astype(bf)
    x3 = (r1 - x2.astype(jnp.float32)).astype(bf)
    return x1, x2, x3


def _dot3(x, e, dims):
    out = None
    for part in _split3(x):
        term = lax.dot_general(part, e, dims, preferred_element_type=jnp.float32)
        out = term if out is None else out + term
    return out


ROWS = (((1,), (0,)), ((), ()))


def _sum_kernel(pop_ref, g1_ref, o_ref):
    for b in range(pop_ref.shape[0]):
        x = pop_ref[b]
        folded = x[:, 0:128]
        for j in range(1, x.shape[1] // 128):
            folded = folded + x[:, j * 128:(j + 1) * 128]
        o_ref[b] = _dot3(folded, g1_ref[...], ROWS)


def _margin_kernel(pop_ref, s2t_ref, e2t_ref, o_ref):
    for b in range(pop_ref.shape[0]):
        o_ref[b] = _dot3(pop_ref[b] * s2t_ref[...], e2t_ref[...], ROWS)


def _fit_kernel(pop_ref, r_ref, s2t_ref, e2_ref, o_ref):
    for b in range(pop_ref.shape[0]):
        rep = _dot3(r_ref[b], e2_ref[...], ROWS)
        o_ref[b] = pop_ref[b] * s2t_ref[...] * rep


def _table_call(kernel, table, smalls, consts, out_last):
    count, rows, width = table.shape
    grid = (count // BLOCK,)
    specs = [pl.BlockSpec((BLOCK, rows, width), lambda i: (i, 0, 0))]
    specs += [pl.BlockSpec((BLOCK,) + x.shape[1:], lambda i: (i, 0, 0)) for x in smalls]
    specs += [pl.BlockSpec(c.shape, lambda i: (0, 0)) for c in consts]
    return pl.pallas_call(
        kernel,
        grid=grid,
        in_specs=specs,
        out_specs=pl.BlockSpec((BLOCK, rows, out_last), lambda i: (i, 0, 0)),
        out_shape=jax.ShapeDtypeStruct((count, rows, out_last), jnp.float32),
    )(table, *smalls, *consts)


def _partner(i, bit):
    if bit in (4, 16, 64):
        low = bit // 2
        r = (i // low) % 4
        return i + ((3 - r) - r) * low
    return i ^ bit


def _xor(x, n, bit):
    return lax.ppermute(x, AXES, [(i, _partner(i, bit)) for i in range(n)])


def make_body(n):
    cols = n // MEMBERS

    def body(population, area_target, national_target, zone_target, area_zone, zone_order):
        count = population.shape[0]
        rows = zone_target.shape[0]
        zones = zone_order.shape[0]
        width = zone_target.shape[1]
        most = count
        pool_rows = rows * MEMBERS
        assert ZONE_MOST < count and (AGE * SEX * HH * TU) % width == 0 and 2 * cols <= width
        f32 = jnp.float32
        idx = lax.axis_index(AXES)
        col, mem = idx // MEMBERS, idx % MEMBERS

        labels = jnp.arange(zones, dtype=jnp.int32)

        def slot_of(z):
            return jnp.sum(jnp.where(zone_order[None, :] == z.reshape(-1)[:, None], labels[None, :], 0), axis=1).reshape(z.shape)

        zlo = area_zone[0]
        zhi = area_zone[count - 1]
        ks = jnp.arange(most, dtype=jnp.int32)
        lanes = jnp.arange(width, dtype=jnp.int32)

        m_kz = zlo + ks
        m_valid = m_kz <= zhi
        m_slot = slot_of(jnp.minimum(m_kz, zones - 1))
        m_mem = (m_slot // rows) % MEMBERS
        m_rank = jnp.sum(((m_mem[:, None] == m_mem[None, :]) & m_valid[None, :] & (ks[None, :] < ks[:, None])).astype(jnp.int32), axis=1)
        over = jnp.any(m_valid & (m_rank >= ROOMY)).astype(f32)

        bf = jnp.bfloat16
        g1 = jnp.asarray(np.arange(128)[:, None] % (HH * TU) == np.arange(HH * TU)[None, :], bf)
        e2_np = np.arange(INC * HH * TU)[None, :] // (HH * TU) == np.arange(INC)[:, None]
        e2 = jnp.asarray(e2_np, bf)
        e2t = jnp.asarray(e2_np.T, bf)
        t1 = _table_call(_sum_kernel, population, [], [g1], HH * TU)
        area_sum = jnp.sum(t1, axis=2)
        s1 = area_target / area_sum
        part = jnp.sum(t1 * s1[:, :, None], axis=0)
        nat_rows = (AGE * SEX * HH * TU) // width

        nat = part.reshape(nat_rows, width)
        flag = jnp.where(lanes == 0, over, 0.0)[None]
        pool = zone_target
        bit = MEMBERS
        while bit < n:
            if pool.shape[0] < SHIP_APART:
                got = _xor(jnp.concatenate([nat, flag, pool], axis=0), n, bit)
                theirs = got[nat_rows + 1:]
            else:
                got = _xor(jnp.concatenate([nat, flag], axis=0), n, bit)
                theirs = _xor(pool, n, bit)
            nat = nat + got[:nat_rows]
            flag = flag + got[nat_rows:nat_rows + 1]
            pool = jnp.where((idx & bit) == 0, jnp.concatenate([pool, theirs], 0), jnp.concatenate([theirs, pool], 0))
            bit *= 2

        zrow = jnp.where(lanes == 2 * mem, zlo.astype(f32), 0.0) + jnp.where(lanes == 2 * mem + 1, zhi.astype(f32), 0.0)
        msg = jnp.concatenate([nat, flag, zrow[None]], axis=0)
        bit = 1
        while bit < MEMBERS:
            msg = msg + _xor(msg, n, bit)
            bit *= 2
        nat = msg[:nat_rows]
        total_over = msg[nat_rows, 0]
        zinfo = msg[nat_rows + 1, : 2 * MEMBERS].reshape(MEMBERS, 2).astype(jnp.int32)
        s2 = national_target / nat.reshape(AGE * SEX, HH * TU)

        c_kz = zinfo[:, 0:1] + ks[None, :]
        c_valid = c_kz <= zinfo[:, 1:2]
        c_slot = slot_of(jnp.minimum(c_kz, zones - 1))
        c_mem = (c_slot // rows) % MEMBERS
        earlier = (c_mem[:, :, None] == c_mem[:, None, :]) & c_valid[:, None, :] & (ks[None, None, :] < ks[None, :, None])
        c_rank = jnp.sum(earlier.astype(jnp.int32), axis=2)
        mine = c_valid & (c_mem == mem)
        c_at = (c_slot // (rows * MEMBERS)) * rows + c_slot % rows

        def exchange(room, low):
            rank = c_rank - low
            hit = (mine & (rank >= 0) & (rank < room))[:, :, None] & (rank[:, :, None] == jnp.arange(room, dtype=jnp.int32)[None, None, :])
            at = jnp.sum(jnp.where(hit, c_at[:, :, None], 0), axis=1)
            sent = jnp.take(pool, at.reshape(-1), axis=0).reshape(MEMBERS, room, width)
            return lax.all_to_all(sent, "mem", 0, 0, tiled=True)

        fast = exchange(ROOMY, 0)
        spare = most - ROOMY
        slow = lax.cond(total_over > 0, lambda: exchange(spare, ROOMY), lambda: jnp.zeros((MEMBERS, spare, width), f32))
        target = jnp.where((m_rank < ROOMY)[:, None], fast[m_mem, jnp.minimum(m_rank, ROOMY - 1)],
                           slow[m_mem, jnp.clip(m_rank - ROOMY, 0, spare - 1)])

        s2t = jnp.tile(s2, (1, INC))
        am = _table_call(_margin_kernel, population, [], [s2t, e2t], INC) * s1[:, :, None]
        am = jnp.sum(am.reshape(count, AGE, SEX, INC), axis=2).reshape(count, AGE * INC)
        k_a = area_zone - zlo
        onehot = (k_a[:, None] == ks[None, :]).astype(f32)
        zp = jnp.sum(onehot[:, :, None] * am[:, None, :], axis=0)
        nk = zhi - zlo
        right = [(i, i + 1) for i in range(n - 1)]
        left = [(i, i - 1) for i in range(1, n)]
        to_right = jnp.stack([zp[nk], jnp.where(lanes == 0, zhi.astype(f32), -1.0)])
        to_left = jnp.stack([zp[0], jnp.where(lanes == 0, zlo.astype(f32), -1.0)])
        from_left = lax.ppermute(to_right, AXES, right)
        from_right = lax.ppermute(to_left, AXES, left)
        zp = zp.at[0].add(jnp.where((from_left[1, 0] == zlo.astype(f32)) & (idx > 0), from_left[0], 0.0))
        zp = zp.at[nk].add(jnp.where((from_right[1, 0] == zhi.astype(f32)) & (idx < n - 1), from_right[0], 0.0))
        ratio = target / zp
        ratio_a = jnp.take(ratio, k_a, axis=0)

        r96 = jnp.repeat(ratio_a.reshape(count, AGE, INC), SEX, axis=1) * s1[:, :, None]
        return _table_call(_fit_kernel, population, [r96], [s2t, e2], INC * HH * TU)

    return body


def solution(mesh):
    n = mesh.shape["area"]
    grid = Mesh(np.asarray(mesh.devices).reshape(n // MEMBERS, MEMBERS), AXES)
    placed = (P(AXES, None, None), P(AXES, None), P(), P(AXES, None), P(AXES), P())
    return jax.shard_map(
        make_body(n), mesh=grid, in_specs=placed, out_specs=P(AXES, None, None), check_vma=False
    )
```

```python
import jax
import jax.numpy as jnp
import numpy as np
from jax import lax
from jax.experimental import pallas as pl
from jax.sharding import Mesh, PartitionSpec as P

AGE = 48
SEX = 2
INC = 32
HH = 8
TU = 4
ZONE_MOST = 6
MEMBERS = 8
ROOMY = 6
AXES = ("col", "mem")
SHIP_APART = 32


HI = lax.Precision.HIGHEST
BLOCK = 4
LANES = (((1,), (1,)), ((), ()))


def _split3(x):
    bf = jnp.bfloat16
    x1 = x.astype(bf)
    r1 = x - x1.astype(jnp.float32)
    x2 = r1.astype(bf)
    x3 = (r1 - x2.astype(jnp.float32)).astype(bf)
    return x1, x2, x3


def _dot3(x, e, dims):
    out = None
    for part in _split3(x):
        term = lax.dot_general(part, e, dims, preferred_element_type=jnp.float32)
        out = term if out is None else out + term
    return out


ROWS = (((1,), (0,)), ((), ()))


def _sum_kernel(pop_ref, g1_ref, o_ref):
    for b in range(pop_ref.shape[0]):
        x = pop_ref[b]
        folded = x[:, 0:128]
        for j in range(1, x.shape[1] // 128):
            folded = folded + x[:, j * 128:(j + 1) * 128]
        o_ref[b] = _dot3(folded, g1_ref[...], ROWS)


def _scale_kernel(pop_ref, at_ref, g1_ref, s1_ref, part_ref):
    @pl.when(pl.program_id(0) == 0)
    def _():
        part_ref[...] = jnp.zeros_like(part_ref)

    acc = part_ref[...]
    for b in range(pop_ref.shape[0]):
        x = pop_ref[b]
        folded = x[:, 0:128]
        for j in range(1, x.shape[1] // 128):
            folded = folded + x[:, j * 128:(j + 1) * 128]
        t = _dot3(folded, g1_ref[...], ROWS)
        s1 = at_ref[b] / jnp.sum(t, axis=1, keepdims=True)
        s1_ref[b] = s1
        acc = acc + t * s1
    part_ref[...] = acc


def _margin_kernel(pop_ref, s2t_ref, e2t_ref, o_ref):
    for b in range(pop_ref.shape[0]):
        o_ref[b] = _dot3(pop_ref[b] * s2t_ref[...], e2t_ref[...], ROWS)


def _fit_kernel(pop_ref, r_ref, s2t_ref, e2_ref, o_ref):
    for b in range(pop_ref.shape[0]):
        rep = _dot3(r_ref[b], e2_ref[...], ROWS)
        o_ref[b] = pop_ref[b] * s2t_ref[...] * rep


def _table_call(kernel, table, smalls, consts, out_last):
    count, rows, width = table.shape
    grid = (count // BLOCK,)
    specs = [pl.BlockSpec((BLOCK, rows, width), lambda i: (i, 0, 0))]
    specs += [pl.BlockSpec((BLOCK,) + x.shape[1:], lambda i: (i, 0, 0)) for x in smalls]
    specs += [pl.BlockSpec(c.shape, lambda i: (0, 0)) for c in consts]
    return pl.pallas_call(
        kernel,
        grid=grid,
        in_specs=specs,
        out_specs=pl.BlockSpec((BLOCK, rows, out_last), lambda i: (i, 0, 0)),
        out_shape=jax.ShapeDtypeStruct((count, rows, out_last), jnp.float32),
    )(table, *smalls, *consts)


def _partner(i, bit):
    if bit in (4, 16, 64):
        low = bit // 2
        r = (i // low) % 4
        return i + ((3 - r) - r) * low
    return i ^ bit


def _xor(x, n, bit):
    return lax.ppermute(x, AXES, [(i, _partner(i, bit)) for i in range(n)])


def make_body(n):
    cols = n // MEMBERS

    def body(population, area_target, national_target, zone_target, area_zone, zone_order):
        count = population.shape[0]
        rows = zone_target.shape[0]
        zones = zone_order.shape[0]
        width = zone_target.shape[1]
        most = count
        pool_rows = rows * MEMBERS
        assert ZONE_MOST < count and (AGE * SEX * HH * TU) % width == 0 and 2 * cols <= width
        f32 = jnp.float32
        idx = lax.axis_index(AXES)
        col, mem = idx // MEMBERS, idx % MEMBERS

        labels = jnp.arange(zones, dtype=jnp.int32)

        def slot_of(z):
            return jnp.sum(jnp.where(zone_order[None, :] == z.reshape(-1)[:, None], labels[None, :], 0), axis=1).reshape(z.shape)

        zlo = area_zone[0]
        zhi = area_zone[count - 1]
        ks = jnp.arange(most, dtype=jnp.int32)
        lanes = jnp.arange(width, dtype=jnp.int32)

        m_kz = zlo + ks
        m_valid = m_kz <= zhi
        m_slot = slot_of(jnp.minimum(m_kz, zones - 1))
        m_mem = (m_slot // rows) % MEMBERS
        m_rank = jnp.sum(((m_mem[:, None] == m_mem[None, :]) & m_valid[None, :] & (ks[None, :] < ks[:, None])).astype(jnp.int32), axis=1)
        over = jnp.any(m_valid & (m_rank >= ROOMY)).astype(f32)

        bf = jnp.bfloat16
        g1 = jnp.asarray(np.arange(128)[:, None] % (HH * TU) == np.arange(HH * TU)[None, :], bf)
        e2_np = np.arange(INC * HH * TU)[None, :] // (HH * TU) == np.arange(INC)[:, None]
        e2 = jnp.asarray(e2_np, bf)
        e2t = jnp.asarray(e2_np.T, bf)
        s1c, part = pl.pallas_call(
            _scale_kernel,
            grid=(count // BLOCK,),
            in_specs=[pl.BlockSpec((BLOCK, AGE * SEX, INC * HH * TU), lambda i: (i, 0, 0)),
                      pl.BlockSpec((BLOCK, AGE * SEX, 1), lambda i: (i, 0, 0)),
                      pl.BlockSpec(g1.shape, lambda i: (0, 0))],
            out_specs=[pl.BlockSpec((BLOCK, AGE * SEX, 1), lambda i: (i, 0, 0)),
                       pl.BlockSpec((AGE * SEX, HH * TU), lambda i: (0, 0))],
            out_shape=[jax.ShapeDtypeStruct((count, AGE * SEX, 1), f32),
                       jax.ShapeDtypeStruct((AGE * SEX, HH * TU), f32)],
        )(population, area_target[:, :, None], g1)
        s1 = s1c[:, :, 0]
        nat_rows = (AGE * SEX * HH * TU) // width

        nat = part.reshape(nat_rows, width)
        flag = jnp.where(lanes == 0, over, 0.0)[None]
        pool = zone_target
        bit = MEMBERS
        while bit < n:
            if pool.shape[0] < SHIP_APART:
                got = _xor(jnp.concatenate([nat, flag, pool], axis=0), n, bit)
                theirs = got[nat_rows + 1:]
            else:
                got = _xor(jnp.concatenate([nat, flag], axis=0), n, bit)
                theirs = _xor(pool, n, bit)
            nat = nat + got[:nat_rows]
            flag = flag + got[nat_rows:nat_rows + 1]
            pool = jnp.where((idx & bit) == 0, jnp.concatenate([pool, theirs], 0), jnp.concatenate([theirs, pool], 0))
            bit *= 2

        zrow = jnp.where(lanes == 2 * mem, zlo.astype(f32), 0.0) + jnp.where(lanes == 2 * mem + 1, zhi.astype(f32), 0.0)
        msg = jnp.concatenate([nat, flag, zrow[None]], axis=0)
        bit = 1
        while bit < MEMBERS:
            msg = msg + _xor(msg, n, bit)
            bit *= 2
        nat = msg[:nat_rows]
        total_over = msg[nat_rows, 0]
        zinfo = msg[nat_rows + 1, : 2 * MEMBERS].reshape(MEMBERS, 2).astype(jnp.int32)
        s2 = national_target / nat.reshape(AGE * SEX, HH * TU)

        c_kz = zinfo[:, 0:1] + ks[None, :]
        c_valid = c_kz <= zinfo[:, 1:2]
        c_slot = slot_of(jnp.minimum(c_kz, zones - 1))
        c_mem = (c_slot // rows) % MEMBERS
        earlier = (c_mem[:, :, None] == c_mem[:, None, :]) & c_valid[:, None, :] & (ks[None, None, :] < ks[None, :, None])
        c_rank = jnp.sum(earlier.astype(jnp.int32), axis=2)
        mine = c_valid & (c_mem == mem)
        c_at = (c_slot // (rows * MEMBERS)) * rows + c_slot % rows

        def exchange(room, low):
            rank = c_rank - low
            hit = (mine & (rank >= 0) & (rank < room))[:, :, None] & (rank[:, :, None] == jnp.arange(room, dtype=jnp.int32)[None, None, :])
            at = jnp.sum(jnp.where(hit, c_at[:, :, None], 0), axis=1)
            sent = jnp.take(pool, at.reshape(-1), axis=0).reshape(MEMBERS, room, width)
            return lax.all_to_all(sent, "mem", 0, 0, tiled=True)

        fast = exchange(ROOMY, 0)
        spare = most - ROOMY
        slow = lax.cond(total_over > 0, lambda: exchange(spare, ROOMY), lambda: jnp.zeros((MEMBERS, spare, width), f32))
        target = jnp.where((m_rank < ROOMY)[:, None], fast[m_mem, jnp.minimum(m_rank, ROOMY - 1)],
                           slow[m_mem, jnp.clip(m_rank - ROOMY, 0, spare - 1)])

        s2t = jnp.tile(s2, (1, INC))
        am = _table_call(_margin_kernel, population, [], [s2t, e2t], INC) * s1[:, :, None]
        am = jnp.sum(am.reshape(count, AGE, SEX, INC), axis=2).reshape(count, AGE * INC)
        k_a = area_zone - zlo
        onehot = (k_a[:, None] == ks[None, :]).astype(f32)
        zp = jnp.sum(onehot[:, :, None] * am[:, None, :], axis=0)
        nk = zhi - zlo
        right = [(i, i + 1) for i in range(n - 1)]
        left = [(i, i - 1) for i in range(1, n)]
        to_right = jnp.stack([zp[nk], jnp.where(lanes == 0, zhi.astype(f32), -1.0)])
        to_left = jnp.stack([zp[0], jnp.where(lanes == 0, zlo.astype(f32), -1.0)])
        from_left = lax.ppermute(to_right, AXES, right)
        from_right = lax.ppermute(to_left, AXES, left)
        zp = zp.at[0].add(jnp.where((from_left[1, 0] == zlo.astype(f32)) & (idx > 0), from_left[0], 0.0))
        zp = zp.at[nk].add(jnp.where((from_right[1, 0] == zhi.astype(f32)) & (idx < n - 1), from_right[0], 0.0))
        ratio = target / zp
        ratio_a = jnp.take(ratio, k_a, axis=0)

        r96 = jnp.repeat(ratio_a.reshape(count, AGE, INC), SEX, axis=1) * s1[:, :, None]
        return _table_call(_fit_kernel, population, [r96], [s2t, e2], INC * HH * TU)

    return body


def solution(mesh):
    n = mesh.shape["area"]
    grid = Mesh(np.asarray(mesh.devices).reshape(n // MEMBERS, MEMBERS), AXES)
    placed = (P(AXES, None, None), P(AXES, None), P(), P(AXES, None), P(AXES), P())
    return jax.shard_map(
        make_body(n), mesh=grid, in_specs=placed, out_specs=P(AXES, None, None), check_vma=False
    )
```

```python
import jax
import jax.numpy as jnp
import numpy as np
from jax import lax
from jax.experimental import pallas as pl
from jax.sharding import Mesh, PartitionSpec as P

AGE = 48
SEX = 2
INC = 32
HH = 8
TU = 4
ZONE_MOST = 6
MEMBERS = 8
ROOMY = 6
AXES = ("col", "mem")
SHIP_APART = 32


HI = lax.Precision.HIGHEST
BLOCK = 4
LANES = (((1,), (1,)), ((), ()))


def _split3(x):
    bf = jnp.bfloat16
    x1 = x.astype(bf)
    r1 = x - x1.astype(jnp.float32)
    x2 = r1.astype(bf)
    x3 = (r1 - x2.astype(jnp.float32)).astype(bf)
    return x1, x2, x3


def _dot3(x, e, dims):
    out = None
    for part in _split3(x):
        term = lax.dot_general(part, e, dims, preferred_element_type=jnp.float32)
        out = term if out is None else out + term
    return out


ROWS = (((1,), (0,)), ((), ()))


def _sum_kernel(pop_ref, g1_ref, o_ref):
    for b in range(pop_ref.shape[0]):
        x = pop_ref[b]
        folded = x[:, 0:128]
        for j in range(1, x.shape[1] // 128):
            folded = folded + x[:, j * 128:(j + 1) * 128]
        o_ref[b] = _dot3(folded, g1_ref[...], ROWS)


def _scale_kernel(pop_ref, at_ref, g1_ref, s1_ref, part_ref):
    @pl.when(pl.program_id(0) == 0)
    def _():
        part_ref[...] = jnp.zeros_like(part_ref)

    acc = part_ref[...]
    for b in range(pop_ref.shape[0]):
        x = pop_ref[b]
        folded = x[:, 0:128]
        for j in range(1, x.shape[1] // 128):
            folded = folded + x[:, j * 128:(j + 1) * 128]
        t = _dot3(folded, g1_ref[...], ROWS)
        s1 = at_ref[b] / jnp.sum(t, axis=1, keepdims=True)
        s1_ref[b] = s1
        acc = acc + t * s1
    part_ref[...] = acc


def _margin_kernel(pop_ref, s1_ref, s2t_ref, e2t_ref, pair_ref, o_ref):
    for b in range(pop_ref.shape[0]):
        o = _dot3(pop_ref[b] * s2t_ref[...], e2t_ref[...], ROWS) * s1_ref[b]
        o_ref[b] = jnp.dot(pair_ref[...], o, precision=HI, preferred_element_type=jnp.float32)


def _fit_kernel(pop_ref, r_ref, s2t_ref, e2_ref, o_ref):
    for b in range(pop_ref.shape[0]):
        rep = _dot3(r_ref[b], e2_ref[...], ROWS)
        o_ref[b] = pop_ref[b] * s2t_ref[...] * rep


def _table_call(kernel, table, smalls, consts, out_last):
    count, rows, width = table.shape
    grid = (count // BLOCK,)
    specs = [pl.BlockSpec((BLOCK, rows, width), lambda i: (i, 0, 0))]
    specs += [pl.BlockSpec((BLOCK,) + x.shape[1:], lambda i: (i, 0, 0)) for x in smalls]
    specs += [pl.BlockSpec(c.shape, lambda i: (0, 0)) for c in consts]
    return pl.pallas_call(
        kernel,
        grid=grid,
        in_specs=specs,
        out_specs=pl.BlockSpec((BLOCK, rows, out_last), lambda i: (i, 0, 0)),
        out_shape=jax.ShapeDtypeStruct((count, rows, out_last), jnp.float32),
    )(table, *smalls, *consts)


def _partner(i, bit):
    if bit in (4, 16, 64):
        low = bit // 2
        r = (i // low) % 4
        return i + ((3 - r) - r) * low
    return i ^ bit


def _xor(x, n, bit):
    return lax.ppermute(x, AXES, [(i, _partner(i, bit)) for i in range(n)])


def make_body(n):
    cols = n // MEMBERS

    def body(population, area_target, national_target, zone_target, area_zone, zone_order):
        count = population.shape[0]
        rows = zone_target.shape[0]
        zones = zone_order.shape[0]
        width = zone_target.shape[1]
        most = count
        pool_rows = rows * MEMBERS
        assert ZONE_MOST < count and (AGE * SEX * HH * TU) % width == 0 and 2 * cols <= width
        f32 = jnp.float32
        idx = lax.axis_index(AXES)
        col, mem = idx // MEMBERS, idx % MEMBERS

        labels = jnp.arange(zones, dtype=jnp.int32)

        def slot_of(z):
            return jnp.sum(jnp.where(zone_order[None, :] == z.reshape(-1)[:, None], labels[None, :], 0), axis=1).reshape(z.shape)

        zlo = area_zone[0]
        zhi = area_zone[count - 1]
        ks = jnp.arange(most, dtype=jnp.int32)
        lanes = jnp.arange(width, dtype=jnp.int32)

        m_kz = zlo + ks
        m_valid = m_kz <= zhi
        m_slot = slot_of(jnp.minimum(m_kz, zones - 1))
        m_mem = (m_slot // rows) % MEMBERS
        m_rank = jnp.sum(((m_mem[:, None] == m_mem[None, :]) & m_valid[None, :] & (ks[None, :] < ks[:, None])).astype(jnp.int32), axis=1)
        over = jnp.any(m_valid & (m_rank >= ROOMY)).astype(f32)

        bf = jnp.bfloat16
        g1 = jnp.asarray(np.arange(128)[:, None] % (HH * TU) == np.arange(HH * TU)[None, :], bf)
        e2_np = np.arange(INC * HH * TU)[None, :] // (HH * TU) == np.arange(INC)[:, None]
        e2 = jnp.asarray(e2_np, bf)
        e2t = jnp.asarray(e2_np.T, bf)
        s1c, part = pl.pallas_call(
            _scale_kernel,
            grid=(count // BLOCK,),
            in_specs=[pl.BlockSpec((BLOCK, AGE * SEX, INC * HH * TU), lambda i: (i, 0, 0)),
                      pl.BlockSpec((BLOCK, AGE * SEX, 1), lambda i: (i, 0, 0)),
                      pl.BlockSpec(g1.shape, lambda i: (0, 0))],
            out_specs=[pl.BlockSpec((BLOCK, AGE * SEX, 1), lambda i: (i, 0, 0)),
                       pl.BlockSpec((AGE * SEX, HH * TU), lambda i: (0, 0))],
            out_shape=[jax.ShapeDtypeStruct((count, AGE * SEX, 1), f32),
                       jax.ShapeDtypeStruct((AGE * SEX, HH * TU), f32)],
        )(population, area_target[:, :, None], g1)
        s1 = s1c[:, :, 0]
        nat_rows = (AGE * SEX * HH * TU) // width

        nat = part.reshape(nat_rows, width)
        flag = jnp.where(lanes == 0, over, 0.0)[None]
        pool = zone_target
        bit = MEMBERS
        while bit < n:
            if pool.shape[0] < SHIP_APART:
                got = _xor(jnp.concatenate([nat, flag, pool], axis=0), n, bit)
                theirs = got[nat_rows + 1:]
            else:
                got = _xor(jnp.concatenate([nat, flag], axis=0), n, bit)
                theirs = _xor(pool, n, bit)
            nat = nat + got[:nat_rows]
            flag = flag + got[nat_rows:nat_rows + 1]
            pool = jnp.where((idx & bit) == 0, jnp.concatenate([pool, theirs], 0), jnp.concatenate([theirs, pool], 0))
            bit *= 2

        zrow = jnp.where(lanes == 2 * mem, zlo.astype(f32), 0.0) + jnp.where(lanes == 2 * mem + 1, zhi.astype(f32), 0.0)
        msg = jnp.concatenate([nat, flag, zrow[None]], axis=0)
        bit = 1
        while bit < MEMBERS:
            msg = msg + _xor(msg, n, bit)
            bit *= 2
        nat = msg[:nat_rows]
        total_over = msg[nat_rows, 0]
        zinfo = msg[nat_rows + 1, : 2 * MEMBERS].reshape(MEMBERS, 2).astype(jnp.int32)
        s2 = national_target / nat.reshape(AGE * SEX, HH * TU)

        c_kz = zinfo[:, 0:1] + ks[None, :]
        c_valid = c_kz <= zinfo[:, 1:2]
        c_slot = slot_of(jnp.minimum(c_kz, zones - 1))
        c_mem = (c_slot // rows) % MEMBERS
        earlier = (c_mem[:, :, None] == c_mem[:, None, :]) & c_valid[:, None, :] & (ks[None, None, :] < ks[None, :, None])
        c_rank = jnp.sum(earlier.astype(jnp.int32), axis=2)
        mine = c_valid & (c_mem == mem)
        c_at = (c_slot // (rows * MEMBERS)) * rows + c_slot % rows

        def exchange(room, low):
            rank = c_rank - low
            hit = (mine & (rank >= 0) & (rank < room))[:, :, None] & (rank[:, :, None] == jnp.arange(room, dtype=jnp.int32)[None, None, :])
            at = jnp.sum(jnp.where(hit, c_at[:, :, None], 0), axis=1)
            sent = jnp.take(pool, at.reshape(-1), axis=0).reshape(MEMBERS, room, width)
            return lax.all_to_all(sent, "mem", 0, 0, tiled=True)

        fast = exchange(ROOMY, 0)
        spare = most - ROOMY
        slow = lax.cond(total_over > 0, lambda: exchange(spare, ROOMY), lambda: jnp.zeros((MEMBERS, spare, width), f32))
        target = jnp.where((m_rank < ROOMY)[:, None], fast[m_mem, jnp.minimum(m_rank, ROOMY - 1)],
                           slow[m_mem, jnp.clip(m_rank - ROOMY, 0, spare - 1)])

        s2t = jnp.tile(s2, (1, INC))
        pair = jnp.asarray(np.arange(AGE * SEX)[None, :] // SEX == np.arange(AGE)[:, None], f32)
        am = pl.pallas_call(
            _margin_kernel,
            grid=(count // BLOCK,),
            in_specs=[pl.BlockSpec((BLOCK, AGE * SEX, INC * HH * TU), lambda i: (i, 0, 0)),
                      pl.BlockSpec((BLOCK, AGE * SEX, 1), lambda i: (i, 0, 0)),
                      pl.BlockSpec(s2t.shape, lambda i: (0, 0)),
                      pl.BlockSpec(e2t.shape, lambda i: (0, 0)),
                      pl.BlockSpec(pair.shape, lambda i: (0, 0))],
            out_specs=pl.BlockSpec((BLOCK, AGE, INC), lambda i: (i, 0, 0)),
            out_shape=jax.ShapeDtypeStruct((count, AGE, INC), f32),
        )(population, s1c, s2t, e2t, pair).reshape(count, AGE * INC)
        k_a = area_zone - zlo
        onehot = (k_a[:, None] == ks[None, :]).astype(f32)
        zp = jnp.sum(onehot[:, :, None] * am[:, None, :], axis=0)
        nk = zhi - zlo
        right = [(i, i + 1) for i in range(n - 1)]
        left = [(i, i - 1) for i in range(1, n)]
        to_right = jnp.stack([zp[nk], jnp.where(lanes == 0, zhi.astype(f32), -1.0)])
        to_left = jnp.stack([zp[0], jnp.where(lanes == 0, zlo.astype(f32), -1.0)])
        from_left = lax.ppermute(to_right, AXES, right)
        from_right = lax.ppermute(to_left, AXES, left)
        zp = zp.at[0].add(jnp.where((from_left[1, 0] == zlo.astype(f32)) & (idx > 0), from_left[0], 0.0))
        zp = zp.at[nk].add(jnp.where((from_right[1, 0] == zhi.astype(f32)) & (idx < n - 1), from_right[0], 0.0))
        ratio = target / zp
        ratio_a = jnp.take(ratio, k_a, axis=0)

        r96 = jnp.repeat(ratio_a.reshape(count, AGE, INC), SEX, axis=1) * s1[:, :, None]
        return _table_call(_fit_kernel, population, [r96], [s2t, e2], INC * HH * TU)

    return body


def solution(mesh):
    n = mesh.shape["area"]
    grid = Mesh(np.asarray(mesh.devices).reshape(n // MEMBERS, MEMBERS), AXES)
    placed = (P(AXES, None, None), P(AXES, None), P(), P(AXES, None), P(AXES), P())
    return jax.shard_map(
        make_body(n), mesh=grid, in_specs=placed, out_specs=P(AXES, None, None), check_vma=False
    )
```

```python
import jax
import jax.numpy as jnp
import numpy as np
from jax import lax
from jax.experimental import pallas as pl
from jax.sharding import Mesh, PartitionSpec as P

AGE = 48
SEX = 2
INC = 32
HH = 8
TU = 4
ZONE_MOST = 6
MEMBERS = 8
ROOMY = 6
AXES = ("col", "mem")
SHIP_APART = 64


HI = lax.Precision.HIGHEST
BLOCK = 4
LANES = (((1,), (1,)), ((), ()))


def _split3(x):
    bf = jnp.bfloat16
    x1 = x.astype(bf)
    r1 = x - x1.astype(jnp.float32)
    x2 = r1.astype(bf)
    x3 = (r1 - x2.astype(jnp.float32)).astype(bf)
    return x1, x2, x3


def _dot3(x, e, dims):
    out = None
    for part in _split3(x):
        term = lax.dot_general(part, e, dims, preferred_element_type=jnp.float32)
        out = term if out is None else out + term
    return out


ROWS = (((1,), (0,)), ((), ()))


def _sum_kernel(pop_ref, g1_ref, o_ref):
    for b in range(pop_ref.shape[0]):
        x = pop_ref[b]
        folded = x[:, 0:128]
        for j in range(1, x.shape[1] // 128):
            folded = folded + x[:, j * 128:(j + 1) * 128]
        o_ref[b] = _dot3(folded, g1_ref[...], ROWS)


def _scale_kernel(pop_ref, at_ref, g1_ref, s1_ref, part_ref):
    @pl.when(pl.program_id(0) == 0)
    def _():
        part_ref[...] = jnp.zeros_like(part_ref)

    acc = part_ref[...]
    for b in range(pop_ref.shape[0]):
        x = pop_ref[b]
        folded = x[:, 0:128]
        for j in range(1, x.shape[1] // 128):
            folded = folded + x[:, j * 128:(j + 1) * 128]
        t = _dot3(folded, g1_ref[...], ROWS)
        s1 = at_ref[b] / jnp.sum(t, axis=1, keepdims=True)
        s1_ref[b] = s1
        acc = acc + t * s1
    part_ref[...] = acc


def _margin_kernel(pop_ref, s2t_ref, e2t_ref, o_ref):
    for b in range(pop_ref.shape[0]):
        o_ref[b] = _dot3(pop_ref[b] * s2t_ref[...], e2t_ref[...], ROWS)


def _fit_kernel(pop_ref, r_ref, s2t_ref, e2_ref, o_ref):
    for b in range(pop_ref.shape[0]):
        rep = _dot3(r_ref[b], e2_ref[...], ROWS)
        o_ref[b] = pop_ref[b] * s2t_ref[...] * rep


def _table_call(kernel, table, smalls, consts, out_last):
    count, rows, width = table.shape
    grid = (count // BLOCK,)
    specs = [pl.BlockSpec((BLOCK, rows, width), lambda i: (i, 0, 0))]
    specs += [pl.BlockSpec((BLOCK,) + x.shape[1:], lambda i: (i, 0, 0)) for x in smalls]
    specs += [pl.BlockSpec(c.shape, lambda i: (0, 0)) for c in consts]
    return pl.pallas_call(
        kernel,
        grid=grid,
        in_specs=specs,
        out_specs=pl.BlockSpec((BLOCK, rows, out_last), lambda i: (i, 0, 0)),
        out_shape=jax.ShapeDtypeStruct((count, rows, out_last), jnp.float32),
    )(table, *smalls, *consts)


def _partner(i, bit):
    if bit in (4, 16, 64):
        low = bit // 2
        r = (i // low) % 4
        return i + ((3 - r) - r) * low
    return i ^ bit


def _xor(x, n, bit):
    return lax.ppermute(x, AXES, [(i, _partner(i, bit)) for i in range(n)])


def make_body(n):
    cols = n // MEMBERS

    def body(population, area_target, national_target, zone_target, area_zone, zone_order):
        count = population.shape[0]
        rows = zone_target.shape[0]
        zones = zone_order.shape[0]
        width = zone_target.shape[1]
        most = count
        pool_rows = rows * MEMBERS
        assert ZONE_MOST < count and (AGE * SEX * HH * TU) % width == 0 and 2 * cols <= width
        f32 = jnp.float32
        idx = lax.axis_index(AXES)
        col, mem = idx // MEMBERS, idx % MEMBERS

        labels = jnp.arange(zones, dtype=jnp.int32)

        def slot_of(z):
            return jnp.sum(jnp.where(zone_order[None, :] == z.reshape(-1)[:, None], labels[None, :], 0), axis=1).reshape(z.shape)

        zlo = area_zone[0]
        zhi = area_zone[count - 1]
        ks = jnp.arange(most, dtype=jnp.int32)
        lanes = jnp.arange(width, dtype=jnp.int32)

        m_kz = zlo + ks
        m_valid = m_kz <= zhi
        m_slot = slot_of(jnp.minimum(m_kz, zones - 1))
        m_mem = (m_slot // rows) % MEMBERS
        m_rank = jnp.sum(((m_mem[:, None] == m_mem[None, :]) & m_valid[None, :] & (ks[None, :] < ks[:, None])).astype(jnp.int32), axis=1)
        over = jnp.any(m_valid & (m_rank >= ROOMY)).astype(f32)

        bf = jnp.bfloat16
        g1 = jnp.asarray(np.arange(128)[:, None] % (HH * TU) == np.arange(HH * TU)[None, :], bf)
        e2_np = np.arange(INC * HH * TU)[None, :] // (HH * TU) == np.arange(INC)[:, None]
        e2 = jnp.asarray(e2_np, bf)
        e2t = jnp.asarray(e2_np.T, bf)
        s1c, part = pl.pallas_call(
            _scale_kernel,
            grid=(count // BLOCK,),
            in_specs=[pl.BlockSpec((BLOCK, AGE * SEX, INC * HH * TU), lambda i: (i, 0, 0)),
                      pl.BlockSpec((BLOCK, AGE * SEX, 1), lambda i: (i, 0, 0)),
                      pl.BlockSpec(g1.shape, lambda i: (0, 0))],
            out_specs=[pl.BlockSpec((BLOCK, AGE * SEX, 1), lambda i: (i, 0, 0)),
                       pl.BlockSpec((AGE * SEX, HH * TU), lambda i: (0, 0))],
            out_shape=[jax.ShapeDtypeStruct((count, AGE * SEX, 1), f32),
                       jax.ShapeDtypeStruct((AGE * SEX, HH * TU), f32)],
        )(population, area_target[:, :, None], g1)
        s1 = s1c[:, :, 0]
        nat_rows = (AGE * SEX * HH * TU) // width

        nat = part.reshape(nat_rows, width)
        flag = jnp.where(lanes == 0, over, 0.0)[None]
        pool = zone_target
        bit = MEMBERS
        while bit < n:
            if pool.shape[0] < SHIP_APART:
                got = _xor(jnp.concatenate([nat, flag, pool], axis=0), n, bit)
                theirs = got[nat_rows + 1:]
            else:
                got = _xor(jnp.concatenate([nat, flag], axis=0), n, bit)
                theirs = _xor(pool, n, bit)
            nat = nat + got[:nat_rows]
            flag = flag + got[nat_rows:nat_rows + 1]
            pool = jnp.where((idx & bit) == 0, jnp.concatenate([pool, theirs], 0), jnp.concatenate([theirs, pool], 0))
            bit *= 2

        zrow = jnp.where(lanes == 2 * mem, zlo.astype(f32), 0.0) + jnp.where(lanes == 2 * mem + 1, zhi.astype(f32), 0.0)
        msg = jnp.concatenate([nat, flag, zrow[None]], axis=0)
        bit = 1
        while bit < MEMBERS:
            msg = msg + _xor(msg, n, bit)
            bit *= 2
        nat = msg[:nat_rows]
        total_over = msg[nat_rows, 0]
        zinfo = msg[nat_rows + 1, : 2 * MEMBERS].reshape(MEMBERS, 2).astype(jnp.int32)
        s2 = national_target / nat.reshape(AGE * SEX, HH * TU)

        c_kz = zinfo[:, 0:1] + ks[None, :]
        c_valid = c_kz <= zinfo[:, 1:2]
        c_slot = slot_of(jnp.minimum(c_kz, zones - 1))
        c_mem = (c_slot // rows) % MEMBERS
        earlier = (c_mem[:, :, None] == c_mem[:, None, :]) & c_valid[:, None, :] & (ks[None, None, :] < ks[None, :, None])
        c_rank = jnp.sum(earlier.astype(jnp.int32), axis=2)
        mine = c_valid & (c_mem == mem)
        c_at = (c_slot // (rows * MEMBERS)) * rows + c_slot % rows

        def exchange(room, low):
            rank = c_rank - low
            hit = (mine & (rank >= 0) & (rank < room))[:, :, None] & (rank[:, :, None] == jnp.arange(room, dtype=jnp.int32)[None, None, :])
            at = jnp.sum(jnp.where(hit, c_at[:, :, None], 0), axis=1)
            sent = jnp.take(pool, at.reshape(-1), axis=0).reshape(MEMBERS, room, width)
            return lax.all_to_all(sent, "mem", 0, 0, tiled=True)

        fast = exchange(ROOMY, 0)
        spare = most - ROOMY
        slow = lax.cond(total_over > 0, lambda: exchange(spare, ROOMY), lambda: jnp.zeros((MEMBERS, spare, width), f32))
        target = jnp.where((m_rank < ROOMY)[:, None], fast[m_mem, jnp.minimum(m_rank, ROOMY - 1)],
                           slow[m_mem, jnp.clip(m_rank - ROOMY, 0, spare - 1)])

        s2t = jnp.tile(s2, (1, INC))
        am = _table_call(_margin_kernel, population, [], [s2t, e2t], INC) * s1[:, :, None]
        am = jnp.sum(am.reshape(count, AGE, SEX, INC), axis=2).reshape(count, AGE * INC)
        k_a = area_zone - zlo
        onehot = (k_a[:, None] == ks[None, :]).astype(f32)
        zp = jnp.sum(onehot[:, :, None] * am[:, None, :], axis=0)
        nk = zhi - zlo
        right = [(i, i + 1) for i in range(n - 1)]
        left = [(i, i - 1) for i in range(1, n)]
        to_right = jnp.stack([zp[nk], jnp.where(lanes == 0, zhi.astype(f32), -1.0)])
        to_left = jnp.stack([zp[0], jnp.where(lanes == 0, zlo.astype(f32), -1.0)])
        from_left = lax.ppermute(to_right, AXES, right)
        from_right = lax.ppermute(to_left, AXES, left)
        zp = zp.at[0].add(jnp.where((from_left[1, 0] == zlo.astype(f32)) & (idx > 0), from_left[0], 0.0))
        zp = zp.at[nk].add(jnp.where((from_right[1, 0] == zhi.astype(f32)) & (idx < n - 1), from_right[0], 0.0))
        ratio = target / zp
        ratio_a = jnp.take(ratio, k_a, axis=0)

        r96 = jnp.repeat(ratio_a.reshape(count, AGE, INC), SEX, axis=1) * s1[:, :, None]
        return _table_call(_fit_kernel, population, [r96], [s2t, e2], INC * HH * TU)

    return body


def solution(mesh):
    n = mesh.shape["area"]
    grid = Mesh(np.asarray(mesh.devices).reshape(n // MEMBERS, MEMBERS), AXES)
    placed = (P(AXES, None, None), P(AXES, None), P(), P(AXES, None), P(AXES), P())
    return jax.shard_map(
        make_body(n), mesh=grid, in_specs=placed, out_specs=P(AXES, None, None), check_vma=False
    )
```

```python
import jax
import jax.numpy as jnp
import numpy as np
from jax import lax
from jax.experimental import pallas as pl
from jax.sharding import Mesh, PartitionSpec as P

AGE = 48
SEX = 2
INC = 32
HH = 8
TU = 4
ZONE_MOST = 6
MEMBERS = 8
ROOMY = 6
AXES = ("col", "mem")
SHIP_APART = 64


HI = lax.Precision.HIGHEST
BLOCK = 4
SCALE_BLOCK = 8
LANES = (((1,), (1,)), ((), ()))


def _split3(x):
    bf = jnp.bfloat16
    x1 = x.astype(bf)
    r1 = x - x1.astype(jnp.float32)
    x2 = r1.astype(bf)
    x3 = (r1 - x2.astype(jnp.float32)).astype(bf)
    return x1, x2, x3


def _dot3(x, e, dims):
    out = None
    for part in _split3(x):
        term = lax.dot_general(part, e, dims, preferred_element_type=jnp.float32)
        out = term if out is None else out + term
    return out


ROWS = (((1,), (0,)), ((), ()))


def _sum_kernel(pop_ref, g1_ref, o_ref):
    for b in range(pop_ref.shape[0]):
        x = pop_ref[b]
        folded = x[:, 0:128]
        for j in range(1, x.shape[1] // 128):
            folded = folded + x[:, j * 128:(j + 1) * 128]
        o_ref[b] = _dot3(folded, g1_ref[...], ROWS)


def _scale_kernel(pop_ref, at_ref, g1_ref, s1_ref, part_ref):
    @pl.when(pl.program_id(0) == 0)
    def _():
        part_ref[...] = jnp.zeros_like(part_ref)

    acc = part_ref[...]
    for b in range(pop_ref.shape[0]):
        x = pop_ref[b]
        folded = x[:, 0:128]
        for j in range(1, x.shape[1] // 128):
            folded = folded + x[:, j * 128:(j + 1) * 128]
        t = _dot3(folded, g1_ref[...], ROWS)
        s1 = at_ref[b] / jnp.sum(t, axis=1, keepdims=True)
        s1_ref[b] = s1
        acc = acc + t * s1
    part_ref[...] = acc


def _margin_kernel(pop_ref, s2t_ref, e2t_ref, o_ref):
    for b in range(pop_ref.shape[0]):
        o_ref[b] = _dot3(pop_ref[b] * s2t_ref[...], e2t_ref[...], ROWS)


def _fit_kernel(pop_ref, r_ref, s2t_ref, e2_ref, o_ref):
    for b in range(pop_ref.shape[0]):
        rep = _dot3(r_ref[b], e2_ref[...], ROWS)
        o_ref[b] = pop_ref[b] * s2t_ref[...] * rep


def _table_call(kernel, table, smalls, consts, out_last):
    count, rows, width = table.shape
    grid = (count // BLOCK,)
    specs = [pl.BlockSpec((BLOCK, rows, width), lambda i: (i, 0, 0))]
    specs += [pl.BlockSpec((BLOCK,) + x.shape[1:], lambda i: (i, 0, 0)) for x in smalls]
    specs += [pl.BlockSpec(c.shape, lambda i: (0, 0)) for c in consts]
    return pl.pallas_call(
        kernel,
        grid=grid,
        in_specs=specs,
        out_specs=pl.BlockSpec((BLOCK, rows, out_last), lambda i: (i, 0, 0)),
        out_shape=jax.ShapeDtypeStruct((count, rows, out_last), jnp.float32),
    )(table, *smalls, *consts)


def _partner(i, bit):
    if bit in (4, 16, 64):
        low = bit // 2
        r = (i // low) % 4
        return i + ((3 - r) - r) * low
    return i ^ bit


def _xor(x, n, bit):
    return lax.ppermute(x, AXES, [(i, _partner(i, bit)) for i in range(n)])


def make_body(n):
    cols = n // MEMBERS

    def body(population, area_target, national_target, zone_target, area_zone, zone_order):
        count = population.shape[0]
        rows = zone_target.shape[0]
        zones = zone_order.shape[0]
        width = zone_target.shape[1]
        most = count
        pool_rows = rows * MEMBERS
        assert ZONE_MOST < count and (AGE * SEX * HH * TU) % width == 0 and 2 * cols <= width
        f32 = jnp.float32
        idx = lax.axis_index(AXES)
        col, mem = idx // MEMBERS, idx % MEMBERS

        labels = jnp.arange(zones, dtype=jnp.int32)

        def slot_of(z):
            return jnp.sum(jnp.where(zone_order[None, :] == z.reshape(-1)[:, None], labels[None, :], 0), axis=1).reshape(z.shape)

        zlo = area_zone[0]
        zhi = area_zone[count - 1]
        ks = jnp.arange(most, dtype=jnp.int32)
        lanes = jnp.arange(width, dtype=jnp.int32)

        m_kz = zlo + ks
        m_valid = m_kz <= zhi
        m_slot = slot_of(jnp.minimum(m_kz, zones - 1))
        m_mem = (m_slot // rows) % MEMBERS
        m_rank = jnp.sum(((m_mem[:, None] == m_mem[None, :]) & m_valid[None, :] & (ks[None, :] < ks[:, None])).astype(jnp.int32), axis=1)
        over = jnp.any(m_valid & (m_rank >= ROOMY)).astype(f32)

        bf = jnp.bfloat16
        g1 = jnp.asarray(np.arange(128)[:, None] % (HH * TU) == np.arange(HH * TU)[None, :], bf)
        e2_np = np.arange(INC * HH * TU)[None, :] // (HH * TU) == np.arange(INC)[:, None]
        e2 = jnp.asarray(e2_np, bf)
        e2t = jnp.asarray(e2_np.T, bf)
        s1c, part = pl.pallas_call(
            _scale_kernel,
            grid=(count // SCALE_BLOCK,),
            in_specs=[pl.BlockSpec((SCALE_BLOCK, AGE * SEX, INC * HH * TU), lambda i: (i, 0, 0)),
                      pl.BlockSpec((SCALE_BLOCK, AGE * SEX, 1), lambda i: (i, 0, 0)),
                      pl.BlockSpec(g1.shape, lambda i: (0, 0))],
            out_specs=[pl.BlockSpec((SCALE_BLOCK, AGE * SEX, 1), lambda i: (i, 0, 0)),
                       pl.BlockSpec((AGE * SEX, HH * TU), lambda i: (0, 0))],
            out_shape=[jax.ShapeDtypeStruct((count, AGE * SEX, 1), f32),
                       jax.ShapeDtypeStruct((AGE * SEX, HH * TU), f32)],
        )(population, area_target[:, :, None], g1)
        s1 = s1c[:, :, 0]
        nat_rows = (AGE * SEX * HH * TU) // width

        nat = part.reshape(nat_rows, width)
        flag = jnp.where(lanes == 0, over, 0.0)[None]
        pool = zone_target
        bit = MEMBERS
        while bit < n:
            if pool.shape[0] < SHIP_APART:
                got = _xor(jnp.concatenate([nat, flag, pool], axis=0), n, bit)
                theirs = got[nat_rows + 1:]
            else:
                got = _xor(jnp.concatenate([nat, flag], axis=0), n, bit)
                theirs = _xor(pool, n, bit)
            nat = nat + got[:nat_rows]
            flag = flag + got[nat_rows:nat_rows + 1]
            pool = jnp.where((idx & bit) == 0, jnp.concatenate([pool, theirs], 0), jnp.concatenate([theirs, pool], 0))
            bit *= 2

        zrow = jnp.where(lanes == 2 * mem, zlo.astype(f32), 0.0) + jnp.where(lanes == 2 * mem + 1, zhi.astype(f32), 0.0)
        msg = jnp.concatenate([nat, flag, zrow[None]], axis=0)
        bit = 1
        while bit < MEMBERS:
            msg = msg + _xor(msg, n, bit)
            bit *= 2
        nat = msg[:nat_rows]
        total_over = msg[nat_rows, 0]
        zinfo = msg[nat_rows + 1, : 2 * MEMBERS].reshape(MEMBERS, 2).astype(jnp.int32)
        s2 = national_target / nat.reshape(AGE * SEX, HH * TU)

        c_kz = zinfo[:, 0:1] + ks[None, :]
        c_valid = c_kz <= zinfo[:, 1:2]
        c_slot = slot_of(jnp.minimum(c_kz, zones - 1))
        c_mem = (c_slot // rows) % MEMBERS
        earlier = (c_mem[:, :, None] == c_mem[:, None, :]) & c_valid[:, None, :] & (ks[None, None, :] < ks[None, :, None])
        c_rank = jnp.sum(earlier.astype(jnp.int32), axis=2)
        mine = c_valid & (c_mem == mem)
        c_at = (c_slot // (rows * MEMBERS)) * rows + c_slot % rows

        def exchange(room, low):
            rank = c_rank - low
            hit = (mine & (rank >= 0) & (rank < room))[:, :, None] & (rank[:, :, None] == jnp.arange(room, dtype=jnp.int32)[None, None, :])
            at = jnp.sum(jnp.where(hit, c_at[:, :, None], 0), axis=1)
            sent = jnp.take(pool, at.reshape(-1), axis=0).reshape(MEMBERS, room, width)
            return lax.all_to_all(sent, "mem", 0, 0, tiled=True)

        fast = exchange(ROOMY, 0)
        spare = most - ROOMY
        slow = lax.cond(total_over > 0, lambda: exchange(spare, ROOMY), lambda: jnp.zeros((MEMBERS, spare, width), f32))
        target = jnp.where((m_rank < ROOMY)[:, None], fast[m_mem, jnp.minimum(m_rank, ROOMY - 1)],
                           slow[m_mem, jnp.clip(m_rank - ROOMY, 0, spare - 1)])

        s2t = jnp.tile(s2, (1, INC))
        am = _table_call(_margin_kernel, population, [], [s2t, e2t], INC) * s1[:, :, None]
        am = jnp.sum(am.reshape(count, AGE, SEX, INC), axis=2).reshape(count, AGE * INC)
        k_a = area_zone - zlo
        onehot = (k_a[:, None] == ks[None, :]).astype(f32)
        zp = jnp.sum(onehot[:, :, None] * am[:, None, :], axis=0)
        nk = zhi - zlo
        right = [(i, i + 1) for i in range(n - 1)]
        left = [(i, i - 1) for i in range(1, n)]
        to_right = jnp.stack([zp[nk], jnp.where(lanes == 0, zhi.astype(f32), -1.0)])
        to_left = jnp.stack([zp[0], jnp.where(lanes == 0, zlo.astype(f32), -1.0)])
        from_left = lax.ppermute(to_right, AXES, right)
        from_right = lax.ppermute(to_left, AXES, left)
        zp = zp.at[0].add(jnp.where((from_left[1, 0] == zlo.astype(f32)) & (idx > 0), from_left[0], 0.0))
        zp = zp.at[nk].add(jnp.where((from_right[1, 0] == zhi.astype(f32)) & (idx < n - 1), from_right[0], 0.0))
        ratio = target / zp
        ratio_a = jnp.take(ratio, k_a, axis=0)

        r96 = jnp.repeat(ratio_a.reshape(count, AGE, INC), SEX, axis=1) * s1[:, :, None]
        return _table_call(_fit_kernel, population, [r96], [s2t, e2], INC * HH * TU)

    return body


def solution(mesh):
    n = mesh.shape["area"]
    grid = Mesh(np.asarray(mesh.devices).reshape(n // MEMBERS, MEMBERS), AXES)
    placed = (P(AXES, None, None), P(AXES, None), P(), P(AXES, None), P(AXES), P())
    return jax.shard_map(
        make_body(n), mesh=grid, in_specs=placed, out_specs=P(AXES, None, None), check_vma=False
    )
```
